32 devices in a mesh: dp: 8 (over z, y), pair: 4 (over x, core).
Axes of the slice: x: 2, y: 2, z: 4, core: 2. Of those that a mesh axis runs over, the one named last changes fastest.
Arguments:
- embeddings: float32 [4096, 1024], P(('dp', 'pair'))
- labels: int32 [4096], P(('dp', 'pair')), may hold values from 0 to 31, as said below
Outputs:
- closest: float32 [4096], P(('dp', 'pair'))
The draws below stay inside these ranges and needn't reach their ends.
Inputs may be any that keep to these rules, and one draw needn't show every extreme that they name: labels // 4 is the owning index of dp of a cluster. In each aligned block of 128 documents (the documents of one device) at most 40 documents belong to one owning index; one owning index, drawn from the seed, gets exactly 40 documents of every block.
All inputs are finite; a program needn't handle non-finite values.
Results may differ from the reference program's by a relative error of at most 0.0003.
Values may be sent and summed in bfloat16 or wider, within the bound.
No kernel may reach another device: no remote copies, remote signals or barrier semaphores. Data moves between devices by JAX's collectives and lax.ppermute only.
A program may use at most 64 MiB of HBM per device.

```python
import math
import jax
import jax.numpy as jnp
from jax import lax

D = 1024
ROWS_DEV = 128
CPO = 4
CAP = 40
TOKENS = 4096
CLUSTERS = 32
N_DP = 8
N_PAIR = 4


dup_groups = 32


def routing(key):
    base = jax.random.fold_in(key, 11)
    key_hot, key_block, key_local, key_dup, key_single = jax.random.split(base, 5)
    hot = jax.random.randint(key_hot, (), 0, N_DP)
    pool = jnp.arange((N_DP - 1) * CAP, dtype=jnp.int32) // CAP

    def one_block(block_key):
        key_pick, key_order = jax.random.split(block_key)
        others = jax.random.permutation(key_pick, pool)[:ROWS_DEV - CAP]
        others = jnp.where(others >= hot, others + 1, others)
        owners = jnp.concatenate([jnp.full((CAP,), hot, dtype=jnp.int32), others.astype(jnp.int32)])
        return jax.random.permutation(key_order, owners)
    owners = jax.vmap(one_block)(jax.random.split(key_block, N_DP * N_PAIR)).reshape(-1).astype(jnp.int32)
    positions = jnp.arange(TOKENS, dtype=jnp.int32)
    earliest = jnp.full((N_DP,), TOKENS, dtype=jnp.int32).at[owners].min(positions)
    single_row = positions == earliest[owners]
    singleton_local = jax.random.randint(key_single, (N_DP,), 0, CPO).astype(jnp.int32)
    shift_local = jax.random.randint(key_local, (TOKENS,), 0, CPO - 1).astype(jnp.int32)
    own_single = singleton_local[owners]
    local = jnp.where(single_row, own_single, (own_single + 1 + shift_local) % CPO).astype(jnp.int32)
    dup = jax.random.randint(key_dup, (TOKENS,), 0, dup_groups)
    cluster = (owners * CPO + local).astype(jnp.int32)
    return (cluster, cluster * dup_groups + dup)


def draw_labels(key, part):
    cluster, source = routing(key)
    return cluster


def draw_embeddings(key, part):
    cluster, source = routing(key)
    key_base, key_noise, key_spread = jax.random.split(jax.random.fold_in(key, 23), 3)
    count = CLUSTERS * dup_groups
    base = jax.random.normal(key_base, (count, D), jnp.float32)
    noise = jax.random.normal(key_noise, (TOKENS, D), jnp.float32)
    spread = jnp.exp(jax.random.uniform(key_spread, (TOKENS, 1), jnp.float32, math.log(0.3), math.log(3.0)))
    rows = base[source] + spread * noise
    return rows.astype(jnp.float32)


def setup_inputs(seed: int = 0) -> dict:
    arg_keys = jax.random.split(jax.random.key(seed), 3)
    return {
        "embeddings": draw_embeddings(jax.random.fold_in(arg_keys[2], 71), 0),
        "labels": draw_labels(jax.random.fold_in(arg_keys[2], 71), 0),
    }


def reference(embeddings, labels):
    norm = jnp.sqrt(lax.optimization_barrier(jnp.sum(embeddings * embeddings, axis=1, keepdims=True)) + 1e-06)
    rounded = (embeddings / norm).astype(jnp.bfloat16)
    rounded = lax.optimization_barrier(rounded)
    unit = rounded.astype(jnp.float32)
    owner = (labels // CPO).astype(jnp.int32)
    order = jnp.argsort(owner, stable=True).astype(jnp.int32)
    member = owner[:, None] == jnp.arange(N_DP, dtype=jnp.int32)[None, :]
    counts = lax.optimization_barrier(jnp.sum(member.astype(jnp.int32), axis=0, dtype=jnp.int32))
    starts = (jnp.cumsum(counts, dtype=jnp.int32) - counts).astype(jnp.int32)
    capacity = N_PAIR * N_DP * CAP
    lane = jnp.arange(capacity, dtype=jnp.int32)
    diagonal = lane[:, None] == lane[None, :]

    def per_owner(index):
        position = starts[index] + lane
        valid = lane < counts[index]
        picked = order[jnp.minimum(position, TOKENS - 1)]
        vectors = unit[picked]
        group = jnp.where(valid, labels[picked], -1).astype(jnp.int32)
        score = jnp.dot(vectors, vectors.T, precision=lax.Precision.HIGHEST, preferred_element_type=jnp.float32)
        same = (group[:, None] == group[None, :]) & (group[:, None] >= 0) & jnp.logical_not(diagonal)
        best = lax.optimization_barrier(jnp.max(jnp.where(same, score, jnp.float32(-2.0)), axis=1))
        target = jnp.where(valid, picked, TOKENS).astype(jnp.int32)
        return (target, best)
    targets, bests = lax.map(per_owner, jnp.arange(N_DP, dtype=jnp.int32))
    closest = jnp.full((TOKENS,), -2.0, dtype=jnp.float32)
    return closest.at[targets.reshape(-1)].set(bests.reshape(-1).astype(jnp.float32), mode='drop')
```

```python
import jax
import jax.numpy as jnp
from jax import lax
from jax.sharding import PartitionSpec as P

CPO = 4


floor_value = -2.0


def shards(embeddings, labels):
    rows, width = embeddings.shape
    groups = lax.axis_size("dp")
    peers = lax.axis_size("pair")
    capacity = 5 * rows // (2 * groups)
    chunk = capacity + 1
    norm = jnp.sqrt(jnp.sum(embeddings * embeddings, axis=1, keepdims=True) + 1e-06)
    unit = (embeddings / norm).astype(jnp.bfloat16)
    owner = labels // CPO
    local = labels - owner * CPO
    onehot = (owner[:, None] == jnp.arange(groups, dtype=jnp.int32)[None, :]).astype(jnp.int32)
    rank = jnp.sum(jnp.cumsum(onehot, axis=0) * onehot, axis=1) - 1
    tag = jnp.full((groups, width), -1.0, jnp.bfloat16)
    tag = tag.at[owner, rank].set(local.astype(jnp.bfloat16))
    outgoing = jnp.zeros((groups, chunk, width), jnp.bfloat16).at[owner, rank].set(unit)
    outgoing = outgoing.at[:, capacity, :].set(tag)
    block = lax.all_to_all(outgoing, "dp", split_axis=0, concat_axis=0, tiled=True)
    tiled_block = jnp.broadcast_to(block[None], (peers,) + block.shape).reshape(
        (peers * groups, chunk, width)
    )
    other = lax.all_to_all(tiled_block, "pair", split_axis=0, concat_axis=0, tiled=True)
    other = other.reshape(peers, groups, chunk, width)
    block_labels = block[:, capacity, :chunk].astype(jnp.int32).reshape(groups * chunk)
    other_labels = other[:, :, capacity, :chunk].astype(jnp.int32).reshape(peers * groups * chunk)
    left = block.reshape(groups * chunk, width)
    right = other.reshape(peers * groups * chunk, width)
    score = jnp.einsum("id,jd->ij", left, right, preferred_element_type=jnp.float32)
    lane = jnp.arange(groups * chunk, dtype=jnp.int32)
    own_index = lax.axis_index("pair") * (groups * chunk) + lane
    other_index = jnp.arange(peers * groups * chunk, dtype=jnp.int32)
    same = (
        (block_labels[:, None] == other_labels[None, :])
        & (block_labels[:, None] >= 0)
        & (own_index[:, None] != other_index[None, :])
    )
    best = jnp.max(jnp.where(same, score, floor_value), axis=1)
    returned = lax.all_to_all(
        best.reshape(groups, chunk), "dp", split_axis=0, concat_axis=0, tiled=True
    )
    return returned[owner, rank]


def solution(mesh):
    in_specs = (P(("dp", "pair"), None), P(("dp", "pair")))
    out_specs = P(("dp", "pair"))
    return jax.shard_map(shards, mesh=mesh, in_specs=in_specs, out_specs=out_specs, check_vma=False)
```

```python
import jax
import jax.numpy as jnp
from jax import lax
from jax.sharding import PartitionSpec as P

CPO = 4


floor_value = -2.0


def piece_best(left, left_labels, right, right_labels, exclude_self):
    score = jnp.einsum("id,jd->ij", left, right, preferred_element_type=jnp.float32)
    same = (left_labels[:, None] == right_labels[None, :]) & (left_labels[:, None] >= 0)
    if exclude_self:
        lane = jnp.arange(left.shape[0], dtype=jnp.int32)
        same = same & (lane[:, None] != lane[None, :])
    return jnp.max(jnp.where(same, score, floor_value), axis=1)


def chunk_labels(block, capacity, chunk):
    groups = block.shape[0]
    return block[:, capacity, :chunk].astype(jnp.int32).reshape(groups * chunk)


def shards(embeddings, labels):
    rows, width = embeddings.shape
    groups = lax.axis_size("dp")
    peers = lax.axis_size("pair")
    capacity = 5 * rows // (2 * groups)
    chunk = -(-(capacity + 1) // 16) * 16
    slots = groups * chunk
    norm = jnp.sqrt(jnp.sum(embeddings * embeddings, axis=1, keepdims=True) + 1e-06)
    unit = (embeddings / norm).astype(jnp.bfloat16)
    owner = labels // CPO
    local = labels - owner * CPO
    onehot = (owner[:, None] == jnp.arange(groups, dtype=jnp.int32)[None, :]).astype(jnp.int32)
    rank = jnp.sum(jnp.cumsum(onehot, axis=0) * onehot, axis=1) - 1
    slot = owner * chunk + rank
    place = slot[None, :] == jnp.arange(slots, dtype=jnp.int32)[:, None]
    outgoing = jnp.dot(place.astype(jnp.bfloat16), unit, preferred_element_type=jnp.float32)
    outgoing = outgoing.astype(jnp.bfloat16).reshape(groups, chunk, width)
    tag = jnp.sum(jnp.where(place, local[None, :] + 1, 0), axis=1) - 1
    tag_row = jnp.full((groups, width), -1, jnp.int32).at[:, :chunk].set(tag.reshape(groups, chunk))
    row_id = jnp.arange(chunk, dtype=jnp.int32)
    outgoing = jnp.where(
        (row_id == capacity)[None, :, None], tag_row.astype(jnp.bfloat16)[:, None, :], outgoing
    )
    block = lax.all_to_all(outgoing, "dp", split_axis=0, concat_axis=0, tiled=True)
    pieces = [block]
    bit = peers // 2
    while bit >= 1:
        perm = [(p, p ^ bit) for p in range(peers)]
        pieces = pieces + [lax.ppermute(x, "pair", perm) for x in pieces]
        bit //= 2
    left = block.reshape(slots, width)
    left_labels = chunk_labels(block, capacity, chunk)
    best = None
    for index, piece in enumerate(pieces):
        piece_max = piece_best(
            left,
            left_labels,
            piece.reshape(slots, width),
            chunk_labels(piece, capacity, chunk),
            index == 0,
        )
        best = piece_max if best is None else jnp.maximum(best, piece_max)
    returned = lax.all_to_all(
        best.reshape(groups, chunk), "dp", split_axis=0, concat_axis=0, tiled=True
    ).reshape(slots)
    return jnp.sum(jnp.where(place, returned[:, None], 0.0), axis=0)


def solution(mesh):
    in_specs = (P(("dp", "pair"), None), P(("dp", "pair")))
    out_specs = P(("dp", "pair"))
    return jax.shard_map(shards, mesh=mesh, in_specs=in_specs, out_specs=out_specs, check_vma=False)
```

```python
import jax
import jax.numpy as jnp
from jax import lax
from jax.sharding import PartitionSpec as P

CPO = 4


floor_value = -2.0


def piece_best(left, left_labels, right, right_labels, exclude_self):
    score = jnp.einsum("id,jd->ij", left, right, preferred_element_type=jnp.float32)
    same = (left_labels[:, None] == right_labels[None, :]) & (left_labels[:, None] >= 0)
    if exclude_self:
        lane = jnp.arange(left.shape[0], dtype=jnp.int32)
        same = same & (lane[:, None] != lane[None, :])
    return jnp.max(jnp.where(same, score, floor_value), axis=1)


def chunk_labels(block, capacity, chunk):
    groups = block.shape[0]
    return block[:, capacity, :chunk].astype(jnp.int32).reshape(groups * chunk)


def dp_exchange(chunks, groups, direction):
    out = [chunks[0]]
    for k in range(1, groups):
        perm = [(d, (d + direction * k) % groups) for d in range(groups)]
        out.append(lax.ppermute(chunks[k], "dp", perm))
    return out


def pair_gather(x, peers):
    pieces = [x]
    bit = peers // 2
    while bit >= 1:
        perm = [(p, p ^ bit) for p in range(peers)]
        pieces = pieces + [lax.ppermute(y, "pair", perm) for y in pieces]
        bit //= 2
    return pieces


def shards(embeddings, labels):
    rows, width = embeddings.shape
    groups = lax.axis_size("dp")
    peers = lax.axis_size("pair")
    capacity = 5 * rows // (2 * groups)
    chunk = -(-(capacity + 1) // 16) * 16
    slots = groups * chunk
    by_permute = groups <= 16
    norm = jnp.sqrt(jnp.sum(embeddings * embeddings, axis=1, keepdims=True) + 1e-06)
    unit = (embeddings / norm).astype(jnp.bfloat16)
    owner = labels // CPO
    local = labels - owner * CPO
    onehot = (owner[:, None] == jnp.arange(groups, dtype=jnp.int32)[None, :]).astype(jnp.int32)
    rank = jnp.sum(jnp.cumsum(onehot, axis=0) * onehot, axis=1) - 1
    if by_permute:
        dest = (owner - lax.axis_index("dp")) % groups
    else:
        dest = owner
    slot = dest * chunk + rank
    place = slot[None, :] == jnp.arange(slots, dtype=jnp.int32)[:, None]
    outgoing = jnp.dot(place.astype(jnp.bfloat16), unit, preferred_element_type=jnp.float32)
    outgoing = outgoing.astype(jnp.bfloat16).reshape(groups, chunk, width)
    tag = jnp.sum(jnp.where(place, local[None, :] + 1, 0), axis=1) - 1
    tag_row = jnp.full((groups, width), -1, jnp.int32).at[:, :chunk].set(tag.reshape(groups, chunk))
    row_id = jnp.arange(chunk, dtype=jnp.int32)
    outgoing = jnp.where(
        (row_id == capacity)[None, :, None], tag_row.astype(jnp.bfloat16)[:, None, :], outgoing
    )
    if by_permute:
        arrived = dp_exchange([outgoing[k] for k in range(groups)], groups, 1)
        gathered = [pair_gather(c, peers) for c in arrived]
        block = jnp.stack(arrived)
        pieces = [jnp.stack([g[j] for g in gathered]) for j in range(len(gathered[0]))]
    else:
        block = lax.all_to_all(outgoing, "dp", split_axis=0, concat_axis=0, tiled=True)
        pieces = pair_gather(block, peers)
    left = block.reshape(slots, width)
    left_labels = chunk_labels(block, capacity, chunk)
    best = None
    for index, piece in enumerate(pieces):
        piece_max = piece_best(
            left,
            left_labels,
            piece.reshape(slots, width),
            chunk_labels(piece, capacity, chunk),
            index == 0,
        )
        best = piece_max if best is None else jnp.maximum(best, piece_max)
    best = best.reshape(groups, chunk)
    if by_permute:
        returned = jnp.stack(dp_exchange([best[k] for k in range(groups)], groups, -1))
    else:
        returned = lax.all_to_all(best, "dp", split_axis=0, concat_axis=0, tiled=True)
    returned = returned.reshape(slots)
    return jnp.sum(jnp.where(place, returned[:, None], 0.0), axis=0)


def solution(mesh):
    in_specs = (P(("dp", "pair"), None), P(("dp", "pair")))
    out_specs = P(("dp", "pair"))
    return jax.shard_map(shards, mesh=mesh, in_specs=in_specs, out_specs=out_specs, check_vma=False)
```

```python
import jax
import jax.numpy as jnp
from jax import lax
from jax.sharding import PartitionSpec as P

CPO = 4


floor_value = -2.0


def same_cluster(left_labels, right_labels, exclude_self):
    same = (left_labels[:, None] == right_labels[None, :]) & (left_labels[:, None] >= 0)
    if exclude_self:
        lane = jnp.arange(left_labels.shape[0], dtype=jnp.int32)
        same = same & (lane[:, None] != lane[None, :])
    return same


def chunk_labels(block, capacity, chunk):
    groups = block.shape[0]
    return block[:, capacity, :chunk].astype(jnp.int32).reshape(groups * chunk)


def pair_gather(x, peers):
    pieces = [x]
    bit = peers // 2
    while bit >= 1:
        perm = [(p, p ^ bit) for p in range(peers)]
        pieces = pieces + [lax.ppermute(y, "pair", perm) for y in pieces]
        bit //= 2
    return pieces


def shards(embeddings, labels):
    rows, width = embeddings.shape
    groups = lax.axis_size("dp")
    peers = lax.axis_size("pair")
    capacity = 5 * rows // (2 * groups)
    chunk = -(-(capacity + 1) // 16) * 16
    slots = groups * chunk
    half = width // 2
    me = lax.axis_index("dp")
    norm = jnp.sqrt(jnp.sum(embeddings * embeddings, axis=1, keepdims=True) + 1e-06)
    unit = (embeddings / norm).astype(jnp.bfloat16)
    owner = labels // CPO
    local = labels - owner * CPO
    onehot = (owner[:, None] == jnp.arange(groups, dtype=jnp.int32)[None, :]).astype(jnp.int32)
    rank = jnp.sum(jnp.cumsum(onehot, axis=0) * onehot, axis=1) - 1
    slot = owner * chunk + rank
    place = slot[None, :] == jnp.arange(slots, dtype=jnp.int32)[:, None]
    outgoing = jnp.dot(place.astype(jnp.bfloat16), unit, preferred_element_type=jnp.float32)
    outgoing = outgoing.astype(jnp.bfloat16).reshape(groups, chunk, width)
    tag = jnp.sum(jnp.where(place, local[None, :] + 1, 0), axis=1) - 1
    tag_row = jnp.full((groups, width), -1, jnp.int32).at[:, :chunk].set(tag.reshape(groups, chunk))
    row_id = jnp.arange(chunk, dtype=jnp.int32)
    outgoing = jnp.where(
        (row_id == capacity)[None, :, None], tag_row.astype(jnp.bfloat16)[:, None, :], outgoing
    )
    score = None
    pieces_labels = None
    for part in range(2):
        sent = outgoing[:, :, part * half:(part + 1) * half]
        block = lax.all_to_all(sent, "dp", split_axis=0, concat_axis=0, tiled=True)
        pieces = pair_gather(block, peers)
        if part == 0:
            pieces_labels = [chunk_labels(x, capacity, chunk) for x in pieces]
        left = block.reshape(slots, half)
        part_score = [
            jnp.einsum(
                "id,jd->ij", left, x.reshape(slots, half), preferred_element_type=jnp.float32
            )
            for x in pieces
        ]
        score = part_score if score is None else [a + b for a, b in zip(score, part_score)]
    best = None
    for index, (piece_score, right_labels) in enumerate(zip(score, pieces_labels)):
        same = same_cluster(pieces_labels[0], right_labels, index == 0)
        piece_max = jnp.max(jnp.where(same, piece_score, floor_value), axis=1)
        best = piece_max if best is None else jnp.maximum(best, piece_max)
    mine = jnp.arange(groups, dtype=jnp.int32)[:, None, None] == me
    contribution = jnp.where(mine, best.reshape(1, groups, chunk), 0.0)
    returned = lax.psum(contribution, "dp")[:, me, :].reshape(slots)
    return jnp.sum(jnp.where(place, returned[:, None], 0.0), axis=0)


def solution(mesh):
    in_specs = (P(("dp", "pair"), None), P(("dp", "pair")))
    out_specs = P(("dp", "pair"))
    return jax.shard_map(shards, mesh=mesh, in_specs=in_specs, out_specs=out_specs, check_vma=False)
```

```python
import jax
import jax.numpy as jnp
from jax import lax
from jax.sharding import PartitionSpec as P

CPO = 4


floor_value = -2.0


def same_cluster(left_labels, right_labels, exclude_self):
    same = (left_labels[:, None] == right_labels[None, :]) & (left_labels[:, None] >= 0)
    if exclude_self:
        lane = jnp.arange(left_labels.shape[0], dtype=jnp.int32)
        same = same & (lane[:, None] != lane[None, :])
    return same


def chunk_labels(block, capacity, chunk):
    groups = block.shape[0]
    return block[:, capacity, :chunk].astype(jnp.int32).reshape(groups * chunk)


def pair_gather(x, peers):
    pieces = [x]
    bit = peers // 2
    while bit >= 1:
        perm = [(p, p ^ bit) for p in range(peers)]
        pieces = pieces + [lax.ppermute(y, "pair", perm) for y in pieces]
        bit //= 2
    return pieces


def shards(embeddings, labels):
    rows, width = embeddings.shape
    groups = lax.axis_size("dp")
    peers = lax.axis_size("pair")
    capacity = 5 * rows // (2 * groups)
    chunk = -(-(capacity + 1) // 16) * 16
    slots = groups * chunk
    bounds = (0, 3 * width // 4, width) if groups <= 16 else (0, width)
    norm = jnp.sqrt(jnp.sum(embeddings * embeddings, axis=1, keepdims=True) + 1e-06)
    unit = (embeddings / norm).astype(jnp.bfloat16)
    owner = labels // CPO
    local = labels - owner * CPO
    onehot = (owner[:, None] == jnp.arange(groups, dtype=jnp.int32)[None, :]).astype(jnp.int32)
    rank = jnp.sum(jnp.cumsum(onehot, axis=0) * onehot, axis=1) - 1
    slot = owner * chunk + rank
    place = slot[None, :] == jnp.arange(slots, dtype=jnp.int32)[:, None]
    outgoing = jnp.dot(place.astype(jnp.bfloat16), unit, preferred_element_type=jnp.float32)
    outgoing = outgoing.astype(jnp.bfloat16).reshape(groups, chunk, width)
    tag = jnp.sum(jnp.where(place, local[None, :] + 1, 0), axis=1) - 1
    tag_row = jnp.full((groups, width), -1, jnp.int32).at[:, :chunk].set(tag.reshape(groups, chunk))
    row_id = jnp.arange(chunk, dtype=jnp.int32)
    outgoing = jnp.where(
        (row_id == capacity)[None, :, None], tag_row.astype(jnp.bfloat16)[:, None, :], outgoing
    )
    score = None
    pieces_labels = None
    block = None
    for part in range(len(bounds) - 1):
        start, stop = bounds[part], bounds[part + 1]
        sent = outgoing[:, :, start:stop]
        if block is not None:
            sent, block = lax.optimization_barrier((sent, block))
        block = lax.all_to_all(sent, "dp", split_axis=0, concat_axis=0, tiled=True)
        pieces = pair_gather(block, peers)
        if part == 0:
            pieces_labels = [chunk_labels(x, capacity, chunk) for x in pieces]
        left = block.reshape(slots, stop - start)
        part_score = [
            jnp.einsum(
                "id,jd->ij", left, x.reshape(slots, stop - start), preferred_element_type=jnp.float32
            )
            for x in pieces
        ]
        score = part_score if score is None else [a + b for a, b in zip(score, part_score)]
    best = None
    for index, (piece_score, right_labels) in enumerate(zip(score, pieces_labels)):
        same = same_cluster(pieces_labels[0], right_labels, index == 0)
        piece_max = jnp.max(jnp.where(same, piece_score, floor_value), axis=1)
        best = piece_max if best is None else jnp.maximum(best, piece_max)
    returned = lax.all_to_all(
        best.reshape(groups, chunk), "dp", split_axis=0, concat_axis=0, tiled=True
    ).reshape(slots)
    return jnp.sum(jnp.where(place, returned[:, None], 0.0), axis=0)


def solution(mesh):
    in_specs = (P(("dp", "pair"), None), P(("dp", "pair")))
    out_specs = P(("dp", "pair"))
    return jax.shard_map(shards, mesh=mesh, in_specs=in_specs, out_specs=out_specs, check_vma=False)
```

```python
import jax
import jax.numpy as jnp
from jax import lax
from jax.sharding import PartitionSpec as P

CPO = 4


floor_value = -2.0


def piece_best(left, left_labels, right, right_labels, exclude_self):
    score = jnp.einsum("id,jd->ij", left, right, preferred_element_type=jnp.float32)
    same = (left_labels[:, None] == right_labels[None, :]) & (left_labels[:, None] >= 0)
    if exclude_self:
        lane = jnp.arange(left.shape[0], dtype=jnp.int32)
        same = same & (lane[:, None] != lane[None, :])
    return jnp.max(jnp.where(same, score, floor_value), axis=1)


def chunk_labels(block, capacity, chunk):
    groups = block.shape[0]
    return block[:, capacity, :chunk].astype(jnp.int32).reshape(groups * chunk)


def shards(embeddings, labels):
    rows, width = embeddings.shape
    groups = lax.axis_size("dp")
    peers = lax.axis_size("pair")
    capacity = 5 * rows // (2 * groups)
    chunk = -(-(capacity + 1) // 16) * 16
    slots = groups * chunk
    norm = jnp.sqrt(jnp.sum(embeddings * embeddings, axis=1, keepdims=True) + 1e-06)
    unit = (embeddings / norm).astype(jnp.bfloat16)
    owner = lax.shift_right_logical(labels, CPO.bit_length() - 1)
    local = jnp.bitwise_and(labels, CPO - 1)
    onehot = (owner[:, None] == jnp.arange(groups, dtype=jnp.int32)[None, :]).astype(jnp.int32)
    rank = jnp.sum(jnp.cumsum(onehot, axis=0) * onehot, axis=1) - 1
    slot = owner * chunk + rank
    place = slot[None, :] == jnp.arange(slots, dtype=jnp.int32)[:, None]
    outgoing = jnp.dot(place.astype(jnp.bfloat16), unit, preferred_element_type=jnp.float32)
    outgoing = outgoing.astype(jnp.bfloat16).reshape(groups, chunk, width)
    tag = jnp.sum(jnp.where(place, local[None, :] + 1, 0), axis=1) - 1
    tag_row = jnp.pad(tag.reshape(groups, chunk), ((0, 0), (0, width - chunk)), constant_values=-1)
    row_id = jnp.arange(chunk, dtype=jnp.int32)
    outgoing = jnp.where(
        (row_id == capacity)[None, :, None], tag_row.astype(jnp.bfloat16)[:, None, :], outgoing
    )
    block = lax.all_to_all(outgoing, "dp", split_axis=0, concat_axis=0, tiled=True)
    top = peers // 2
    far = lax.ppermute(block, "pair", [(p, p ^ top) for p in range(peers)]) if top else None
    left = block.reshape(slots, width)
    left_labels = chunk_labels(block, capacity, chunk)

    def spread(x):
        pieces = [x]
        bit = top // 2
        while bit >= 1:
            perm = [(p, p ^ bit) for p in range(peers)]
            pieces = pieces + [lax.ppermute(y, "pair", perm) for y in pieces]
            bit //= 2
        return pieces

    def best_over(pieces, first_is_own):
        best = None
        for index, piece in enumerate(pieces):
            piece_max = piece_best(
                left,
                left_labels,
                piece.reshape(slots, width),
                chunk_labels(piece, capacity, chunk),
                first_is_own and index == 0,
            )
            best = piece_max if best is None else jnp.maximum(best, piece_max)
        return best

    best = best_over(spread(block), True)
    if far is not None:
        far, best = lax.optimization_barrier((far, best))
        best = jnp.maximum(best, best_over(spread(far), False))
    returned = lax.all_to_all(
        best.reshape(groups, 1, chunk), "dp", split_axis=0, concat_axis=0, tiled=True
    ).reshape(slots)
    return jnp.sum(jnp.where(place, returned[:, None], 0.0), axis=0)


def solution(mesh):
    in_specs = (P(("dp", "pair"), None), P(("dp", "pair")))
    out_specs = P(("dp", "pair"))
    return jax.shard_map(shards, mesh=mesh, in_specs=in_specs, out_specs=out_specs, check_vma=False)
```

```python
import jax
import jax.numpy as jnp
from jax import lax
from jax.sharding import PartitionSpec as P

CPO = 4


floor_value = -2.0


def piece_best(left, left_labels, right, right_labels, exclude_self):
    score = jnp.einsum("id,jd->ij", left, right, preferred_element_type=jnp.float32)
    same = (left_labels[:, None] == right_labels[None, :]) & (left_labels[:, None] >= 0)
    if exclude_self:
        lane = jnp.arange(left.shape[0], dtype=jnp.int32)
        same = same & (lane[:, None] != lane[None, :])
    return jnp.max(jnp.where(same, score, floor_value), axis=1)


def chunk_labels(block, capacity, chunk):
    groups = block.shape[0]
    return block[:, capacity, :chunk].astype(jnp.int32).reshape(groups * chunk)


def shards(embeddings, labels):
    rows, width = embeddings.shape
    groups = lax.axis_size("dp")
    peers = lax.axis_size("pair")
    capacity = 5 * rows // (2 * groups)
    chunk = -(-(capacity + 1) // 16) * 16
    slots = groups * chunk
    norm = jnp.sqrt(jnp.sum(embeddings * embeddings, axis=1, keepdims=True) + 1e-06)
    unit = (embeddings / norm).astype(jnp.bfloat16)
    owner = lax.shift_right_logical(labels, CPO.bit_length() - 1)
    local = jnp.bitwise_and(labels, CPO - 1)
    onehot = (owner[:, None] == jnp.arange(groups, dtype=jnp.int32)[None, :]).astype(jnp.int32)
    rank = jnp.sum(jnp.cumsum(onehot, axis=0) * onehot, axis=1) - 1
    slot = owner * chunk + rank
    place = slot[None, :] == jnp.arange(slots, dtype=jnp.int32)[:, None]
    outgoing = jnp.dot(place.astype(jnp.bfloat16), unit, preferred_element_type=jnp.float32)
    outgoing = outgoing.astype(jnp.bfloat16).reshape(groups, chunk, width)
    tag = jnp.sum(jnp.where(place, local[None, :] + 1, 0), axis=1) - 1
    tag_row = jnp.pad(tag.reshape(groups, chunk), ((0, 0), (0, width - chunk)), constant_values=-1)
    row_id = jnp.arange(chunk, dtype=jnp.int32)
    outgoing = jnp.where(
        (row_id == capacity)[None, :, None], tag_row.astype(jnp.bfloat16)[:, None, :], outgoing
    )
    block = lax.all_to_all(outgoing, "dp", split_axis=0, concat_axis=0, tiled=True)
    top = peers // 2
    far = lax.ppermute(block, "pair", [(p, p ^ top) for p in range(peers)]) if top else None
    left = block.reshape(slots, width)
    left_labels = chunk_labels(block, capacity, chunk)

    def spread(x):
        pieces = [x]
        bit = top // 2
        while bit >= 1:
            perm = [(p, p ^ bit) for p in range(peers)]
            pieces = pieces + [lax.ppermute(y, "pair", perm) for y in pieces]
            bit //= 2
        return pieces

    def best_over(pieces, first_is_own):
        best = None
        for index, piece in enumerate(pieces):
            piece_max = piece_best(
                left,
                left_labels,
                piece.reshape(slots, width),
                chunk_labels(piece, capacity, chunk),
                first_is_own and index == 0,
            )
            best = piece_max if best is None else jnp.maximum(best, piece_max)
        return best

    best = best_over(spread(block), True)
    if far is not None:
        far, best = lax.optimization_barrier((far, best))
        best = jnp.maximum(best, best_over(spread(far), False))
    lanes = -(-chunk // 128) * 128
    sent = jnp.pad(best.reshape(groups, 1, chunk), ((0, 0), (0, 7), (0, lanes - chunk)))
    returned = lax.all_to_all(sent, "dp", split_axis=0, concat_axis=0, tiled=True)
    returned = returned[:, 0, :chunk].reshape(slots)
    return jnp.sum(jnp.where(place, returned[:, None], 0.0), axis=0)


def solution(mesh):
    in_specs = (P(("dp", "pair"), None), P(("dp", "pair")))
    out_specs = P(("dp", "pair"))
    return jax.shard_map(shards, mesh=mesh, in_specs=in_specs, out_specs=out_specs, check_vma=False)
```

```python
import functools

import jax
import jax.numpy as jnp
from jax import lax
from jax.experimental import pallas as pl
from jax.experimental.pallas import tpu as pltpu
from jax.sharding import PartitionSpec as P

CPO = 4


floor_value = -2.0


def piece_best(left, left_labels, right, right_labels, exclude_self):
    score = jnp.einsum("id,jd->ij", left, right, preferred_element_type=jnp.float32)
    same = (left_labels[:, None] == right_labels[None, :]) & (left_labels[:, None] >= 0)
    if exclude_self:
        lane = jnp.arange(left.shape[0], dtype=jnp.int32)
        same = same & (lane[:, None] != lane[None, :])
    return jnp.max(jnp.where(same, score, floor_value), axis=1)


def chunk_labels(block, capacity, chunk):
    groups = block.shape[0]
    return block[:, capacity, :chunk].astype(jnp.int32).reshape(groups * chunk)


def prepare_kernel(emb_ref, lrow_ref, lcol_ref, out_ref, slot_ref, *, groups, chunk, capacity):
    rows, width = emb_ref.shape
    slots = groups * chunk
    shift = CPO.bit_length() - 1
    e = emb_ref[...]
    norm = jnp.sqrt(jnp.sum(e * e, axis=1, keepdims=True) + 1e-06)
    unit = (e / norm).astype(jnp.bfloat16)
    lrow = lrow_ref[...]
    lcol = lcol_ref[...]
    orow = lax.shift_right_logical(lrow, shift)
    ocol = lax.shift_right_logical(lcol, shift)
    local_row = jnp.bitwise_and(lrow, CPO - 1)
    first = lax.broadcasted_iota(jnp.int32, (rows, rows), 0)
    second = lax.broadcasted_iota(jnp.int32, (rows, rows), 1)
    same = ocol == orow
    rank_row = jnp.sum(jnp.where(same & (first < second), 1, 0), axis=0, keepdims=True)
    rank_col = jnp.sum(jnp.where(same & (second < first), 1, 0), axis=1, keepdims=True)
    slot_row = orow * chunk + rank_row
    slot_ref[...] = slot_row
    place = (lax.broadcasted_iota(jnp.int32, (slots, rows), 0) == slot_row).astype(jnp.bfloat16)
    placed = jnp.dot(place, unit, preferred_element_type=jnp.float32)
    weight = jnp.where(
        lax.broadcasted_iota(jnp.int32, (groups, rows), 0) == orow, local_row + 1, 0
    ).astype(jnp.bfloat16)
    at_rank = (lax.broadcasted_iota(jnp.int32, (rows, width), 1) == rank_col).astype(jnp.bfloat16)
    tags = jnp.dot(weight, at_rank, preferred_element_type=jnp.float32)
    slot_id = lax.broadcasted_iota(jnp.int32, (slots, groups), 0)
    of_group = (
        lax.div(slot_id, chunk) == lax.broadcasted_iota(jnp.int32, (slots, groups), 1)
    ).astype(jnp.bfloat16)
    tag_rows = jnp.dot(of_group, tags.astype(jnp.bfloat16), preferred_element_type=jnp.float32)
    in_chunk = lax.rem(lax.broadcasted_iota(jnp.int32, (slots, width), 0), chunk)
    out_ref[...] = jnp.where(in_chunk == capacity, tag_rows - 1.0, placed).astype(jnp.bfloat16)


def prepare(embeddings, labels, groups, chunk, capacity):
    rows, width = embeddings.shape
    slots = groups * chunk
    vmem = pltpu.MemorySpace.VMEM
    return pl.pallas_call(
        functools.partial(prepare_kernel, groups=groups, chunk=chunk, capacity=capacity),
        out_shape=(
            jax.ShapeDtypeStruct((slots, width), jnp.bfloat16),
            jax.ShapeDtypeStruct((1, rows), jnp.int32),
        ),
        in_specs=[pl.BlockSpec(memory_space=vmem)] * 3,
        out_specs=(pl.BlockSpec(memory_space=vmem), pl.BlockSpec(memory_space=vmem)),
        cost_estimate=pl.CostEstimate(
            flops=2 * slots * rows * width + 4 * rows * width,
            transcendentals=rows,
            bytes_accessed=rows * width * 4 + slots * width * 2,
        ),
    )(embeddings, labels[None, :], labels[:, None])


def shards(embeddings, labels):
    rows, width = embeddings.shape
    groups = lax.axis_size("dp")
    peers = lax.axis_size("pair")
    capacity = 5 * rows // (2 * groups)
    chunk = -(-(capacity + 1) // 16) * 16
    slots = groups * chunk
    if groups <= 16:
        outgoing, slot = prepare(embeddings, labels, groups, chunk, capacity)
        outgoing = outgoing.reshape(groups, chunk, width)
        slot = slot.reshape(rows)
        place = slot[None, :] == jnp.arange(slots, dtype=jnp.int32)[:, None]
    else:
        norm = jnp.sqrt(jnp.sum(embeddings * embeddings, axis=1, keepdims=True) + 1e-06)
        unit = (embeddings / norm).astype(jnp.bfloat16)
        owner = lax.shift_right_logical(labels, CPO.bit_length() - 1)
        local = jnp.bitwise_and(labels, CPO - 1)
        onehot = (owner[:, None] == jnp.arange(groups, dtype=jnp.int32)[None, :]).astype(jnp.int32)
        rank = jnp.sum(jnp.cumsum(onehot, axis=0) * onehot, axis=1) - 1
        slot = owner * chunk + rank
        place = slot[None, :] == jnp.arange(slots, dtype=jnp.int32)[:, None]
        outgoing = jnp.dot(place.astype(jnp.bfloat16), unit, preferred_element_type=jnp.float32)
        outgoing = outgoing.astype(jnp.bfloat16).reshape(groups, chunk, width)
        tag = jnp.sum(jnp.where(place, local[None, :] + 1, 0), axis=1) - 1
        tag_row = jnp.pad(tag.reshape(groups, chunk), ((0, 0), (0, width - chunk)), constant_values=-1)
        row_id = jnp.arange(chunk, dtype=jnp.int32)
        outgoing = jnp.where(
            (row_id == capacity)[None, :, None], tag_row.astype(jnp.bfloat16)[:, None, :], outgoing
        )
    block = lax.all_to_all(outgoing, "dp", split_axis=0, concat_axis=0, tiled=True)
    top = peers // 2
    far = lax.ppermute(block, "pair", [(p, p ^ top) for p in range(peers)]) if top else None
    left = block.reshape(slots, width)
    left_labels = chunk_labels(block, capacity, chunk)

    def spread(x):
        pieces = [x]
        bit = top // 2
        while bit >= 1:
            perm = [(p, p ^ bit) for p in range(peers)]
            pieces = pieces + [lax.ppermute(y, "pair", perm) for y in pieces]
            bit //= 2
        return pieces

    def best_over(pieces, first_is_own):
        best = None
        for index, piece in enumerate(pieces):
            piece_max = piece_best(
                left,
                left_labels,
                piece.reshape(slots, width),
                chunk_labels(piece, capacity, chunk),
                first_is_own and index == 0,
            )
            best = piece_max if best is None else jnp.maximum(best, piece_max)
        return best

    best = best_over(spread(block), True)
    if far is not None:
        far, best = lax.optimization_barrier((far, best))
        best = jnp.maximum(best, best_over(spread(far), False))
    lanes = -(-chunk // 128) * 128
    sent = jnp.pad(best.reshape(groups, 1, chunk), ((0, 0), (0, 7), (0, lanes - chunk)))
    returned = lax.all_to_all(sent, "dp", split_axis=0, concat_axis=0, tiled=True)
    returned = returned[:, 0, :chunk].reshape(slots)
    return jnp.sum(jnp.where(place, returned[:, None], 0.0), axis=0)


def solution(mesh):
    in_specs = (P(("dp", "pair"), None), P(("dp", "pair")))
    out_specs = P(("dp", "pair"))
    return jax.shard_map(shards, mesh=mesh, in_specs=in_specs, out_specs=out_specs, check_vma=False)
```

```python
import functools

import jax
import jax.numpy as jnp
from jax import lax
from jax.experimental import pallas as pl
from jax.experimental.pallas import tpu as pltpu
from jax.sharding import PartitionSpec as P

CPO = 4


floor_value = -2.0


def piece_best(left, left_labels, right, right_labels, exclude_self):
    score = jnp.einsum("id,jd->ij", left, right, preferred_element_type=jnp.float32)
    same = (left_labels[:, None] == right_labels[None, :]) & (left_labels[:, None] >= 0)
    if exclude_self:
        lane = jnp.arange(left.shape[0], dtype=jnp.int32)
        same = same & (lane[:, None] != lane[None, :])
    return jnp.max(jnp.where(same, score, floor_value), axis=1)


def chunk_labels(block, capacity, chunk):
    groups = block.shape[0]
    return block[:, capacity, :chunk].astype(jnp.int32).reshape(groups * chunk)


def prepare_kernel(emb_ref, lrow_ref, out_ref, slot_ref, *, groups, chunk, capacity):
    rows, width = emb_ref.shape
    slots = groups * chunk
    shift = CPO.bit_length() - 1
    e = emb_ref[...]
    norm = jnp.sqrt(jnp.sum(e * e, axis=1, keepdims=True) + 1e-06)
    unit = (e / norm).astype(jnp.bfloat16)
    lrow = lrow_ref[...]
    orow = lax.shift_right_logical(lrow, shift)
    local_row = jnp.bitwise_and(lrow, CPO - 1)
    first = lax.broadcasted_iota(jnp.int32, (rows, rows), 0)
    second = lax.broadcasted_iota(jnp.int32, (rows, rows), 1)
    ocol = jnp.sum(jnp.where(first == second, orow, 0), axis=1, keepdims=True)
    same = ocol == orow
    rank_row = jnp.sum(jnp.where(same & (first < second), 1, 0), axis=0, keepdims=True)
    rank_col = jnp.sum(jnp.where(same & (second < first), 1, 0), axis=1, keepdims=True)
    slot_row = orow * chunk + rank_row
    slot_ref[...] = slot_row
    place = (lax.broadcasted_iota(jnp.int32, (slots, rows), 0) == slot_row).astype(jnp.bfloat16)
    placed = jnp.dot(place, unit, preferred_element_type=jnp.float32)
    weight = jnp.where(
        lax.broadcasted_iota(jnp.int32, (groups, rows), 0) == orow, local_row + 1, 0
    ).astype(jnp.bfloat16)
    at_rank = (lax.broadcasted_iota(jnp.int32, (rows, width), 1) == rank_col).astype(jnp.bfloat16)
    tags = jnp.dot(weight, at_rank, preferred_element_type=jnp.float32) - 1.0
    tag_slot = lax.broadcasted_iota(jnp.int32, (slots, groups), 1) * chunk + capacity
    at_tag = (lax.broadcasted_iota(jnp.int32, (slots, groups), 0) == tag_slot).astype(jnp.bfloat16)
    placed = placed + jnp.dot(at_tag, tags.astype(jnp.bfloat16), preferred_element_type=jnp.float32)
    out_ref[...] = placed.astype(jnp.bfloat16)


def prepare(embeddings, labels, groups, chunk, capacity):
    rows, width = embeddings.shape
    slots = groups * chunk
    vmem = pltpu.MemorySpace.VMEM
    return pl.pallas_call(
        functools.partial(prepare_kernel, groups=groups, chunk=chunk, capacity=capacity),
        out_shape=(
            jax.ShapeDtypeStruct((slots, width), jnp.bfloat16),
            jax.ShapeDtypeStruct((1, rows), jnp.int32),
        ),
        in_specs=[pl.BlockSpec(memory_space=vmem)] * 2,
        out_specs=(pl.BlockSpec(memory_space=vmem), pl.BlockSpec(memory_space=vmem)),
        cost_estimate=pl.CostEstimate(
            flops=2 * slots * rows * width + 4 * rows * width,
            transcendentals=rows,
            bytes_accessed=rows * width * 4 + slots * width * 2,
        ),
    )(embeddings, labels[None, :])


def shards(embeddings, labels):
    rows, width = embeddings.shape
    groups = lax.axis_size("dp")
    peers = lax.axis_size("pair")
    capacity = 5 * rows // (2 * groups)
    chunk = -(-(capacity + 1) // 16) * 16
    slots = groups * chunk
    if groups <= 16:
        outgoing, slot = prepare(embeddings, labels, groups, chunk, capacity)
        outgoing = outgoing.reshape(groups, chunk, width)
        slot = slot.reshape(rows)
        place = slot[None, :] == jnp.arange(slots, dtype=jnp.int32)[:, None]
    else:
        norm = jnp.sqrt(jnp.sum(embeddings * embeddings, axis=1, keepdims=True) + 1e-06)
        unit = (embeddings / norm).astype(jnp.bfloat16)
        owner = lax.shift_right_logical(labels, CPO.bit_length() - 1)
        local = jnp.bitwise_and(labels, CPO - 1)
        onehot = (owner[:, None] == jnp.arange(groups, dtype=jnp.int32)[None, :]).astype(jnp.int32)
        rank = jnp.sum(jnp.cumsum(onehot, axis=0) * onehot, axis=1) - 1
        slot = owner * chunk + rank
        place = slot[None, :] == jnp.arange(slots, dtype=jnp.int32)[:, None]
        outgoing = jnp.dot(place.astype(jnp.bfloat16), unit, preferred_element_type=jnp.float32)
        outgoing = outgoing.astype(jnp.bfloat16).reshape(groups, chunk, width)
        tag = jnp.sum(jnp.where(place, local[None, :] + 1, 0), axis=1) - 1
        tag_row = jnp.pad(tag.reshape(groups, chunk), ((0, 0), (0, width - chunk)), constant_values=-1)
        row_id = jnp.arange(chunk, dtype=jnp.int32)
        outgoing = jnp.where(
            (row_id == capacity)[None, :, None], tag_row.astype(jnp.bfloat16)[:, None, :], outgoing
        )
    block = lax.all_to_all(outgoing, "dp", split_axis=0, concat_axis=0, tiled=True)
    top = peers // 2
    far = lax.ppermute(block, "pair", [(p, p ^ top) for p in range(peers)]) if top else None
    left = block.reshape(slots, width)
    left_labels = chunk_labels(block, capacity, chunk)

    def spread(x):
        pieces = [x]
        bit = top // 2
        while bit >= 1:
            perm = [(p, p ^ bit) for p in range(peers)]
            pieces = pieces + [lax.ppermute(y, "pair", perm) for y in pieces]
            bit //= 2
        return pieces

    def best_over(pieces, first_is_own):
        best = None
        for index, piece in enumerate(pieces):
            piece_max = piece_best(
                left,
                left_labels,
                piece.reshape(slots, width),
                chunk_labels(piece, capacity, chunk),
                first_is_own and index == 0,
            )
            best = piece_max if best is None else jnp.maximum(best, piece_max)
        return best

    best = best_over(spread(block), True)
    if far is not None:
        far, best = lax.optimization_barrier((far, best))
        best = jnp.maximum(best, best_over(spread(far), False))
    lanes = -(-chunk // 128) * 128
    sent = jnp.pad(best.reshape(groups, 1, chunk), ((0, 0), (0, 7), (0, lanes - chunk)))
    returned = lax.all_to_all(sent, "dp", split_axis=0, concat_axis=0, tiled=True)
    returned = returned[:, 0, :chunk].reshape(slots)
    return jnp.sum(jnp.where(place, returned[:, None], 0.0), axis=0)


def solution(mesh):
    in_specs = (P(("dp", "pair"), None), P(("dp", "pair")))
    out_specs = P(("dp", "pair"))
    return jax.shard_map(shards, mesh=mesh, in_specs=in_specs, out_specs=out_specs, check_vma=False)
```

```python
import functools

import jax
import jax.numpy as jnp
from jax import lax
from jax.experimental import pallas as pl
from jax.experimental.pallas import tpu as pltpu
from jax.sharding import PartitionSpec as P

CPO = 4


floor_value = -2.0


def piece_best(left, left_labels, right, right_labels, exclude_self):
    score = jnp.einsum("id,jd->ij", left, right, preferred_element_type=jnp.float32)
    same = (left_labels[:, None] == right_labels[None, :]) & (left_labels[:, None] >= 0)
    if exclude_self:
        lane = jnp.arange(left.shape[0], dtype=jnp.int32)
        same = same & (lane[:, None] != lane[None, :])
    return jnp.max(jnp.where(same, score, floor_value), axis=1)


def chunk_labels(block, capacity, chunk):
    groups = block.shape[0]
    return block[:, capacity, :chunk].astype(jnp.int32).reshape(groups * chunk)


def prepare_kernel(emb_ref, lrow_ref, out_ref, slot_ref, *, groups, chunk, capacity):
    rows, width = emb_ref.shape
    slots = groups * chunk
    shift = CPO.bit_length() - 1
    e = emb_ref[...]
    norm = jnp.sqrt(jnp.sum(e * e, axis=1, keepdims=True) + 1e-06)
    unit = (e * (1.0 / norm)).astype(jnp.bfloat16)
    lrow = lrow_ref[...]
    orow = lax.shift_right_logical(lrow, shift)
    local_row = jnp.bitwise_and(lrow, CPO - 1)
    first = lax.broadcasted_iota(jnp.int32, (rows, rows), 0)
    second = lax.broadcasted_iota(jnp.int32, (rows, rows), 1)
    ocol = jnp.sum(jnp.where(first == second, orow, 0), axis=1, keepdims=True)
    same = ocol == orow
    rank_row = jnp.sum(jnp.where(same & (first < second), 1, 0), axis=0, keepdims=True)
    rank_col = jnp.sum(jnp.where(same & (second < first), 1, 0), axis=1, keepdims=True)
    slot_row = orow * chunk + rank_row
    slot_ref[...] = slot_row
    place = (lax.broadcasted_iota(jnp.int32, (slots, rows), 0) == slot_row).astype(jnp.bfloat16)
    placed = jnp.dot(place, unit, preferred_element_type=jnp.float32)
    weight = jnp.where(
        lax.broadcasted_iota(jnp.int32, (groups, rows), 0) == orow, local_row + 1, 0
    ).astype(jnp.bfloat16)
    at_rank = (lax.broadcasted_iota(jnp.int32, (rows, width), 1) == rank_col).astype(jnp.bfloat16)
    tags = (jnp.dot(weight, at_rank, preferred_element_type=jnp.float32) - 1.0).astype(jnp.bfloat16)
    out_ref[...] = placed.astype(jnp.bfloat16)
    for g in range(groups):
        out_ref[pl.ds(g * chunk + capacity, 1), :] = tags[g:g + 1, :]


def prepare(embeddings, labels, groups, chunk, capacity):
    rows, width = embeddings.shape
    slots = groups * chunk
    vmem = pltpu.MemorySpace.VMEM
    return pl.pallas_call(
        functools.partial(prepare_kernel, groups=groups, chunk=chunk, capacity=capacity),
        out_shape=(
            jax.ShapeDtypeStruct((slots, width), jnp.bfloat16),
            jax.ShapeDtypeStruct((1, rows), jnp.int32),
        ),
        in_specs=[pl.BlockSpec(memory_space=vmem)] * 2,
        out_specs=(pl.BlockSpec(memory_space=vmem), pl.BlockSpec(memory_space=vmem)),
        cost_estimate=pl.CostEstimate(
            flops=2 * slots * rows * width + 4 * rows * width,
            transcendentals=rows,
            bytes_accessed=rows * width * 4 + slots * width * 2,
        ),
    )(embeddings, labels[None, :])


def shards(embeddings, labels):
    rows, width = embeddings.shape
    groups = lax.axis_size("dp")
    peers = lax.axis_size("pair")
    capacity = 5 * rows // (2 * groups)
    chunk = -(-(capacity + 1) // 16) * 16
    slots = groups * chunk
    if groups <= 16:
        outgoing, slot = prepare(embeddings, labels, groups, chunk, capacity)
        outgoing = outgoing.reshape(groups, chunk, width)
        slot = slot.reshape(rows)
        place = slot[None, :] == jnp.arange(slots, dtype=jnp.int32)[:, None]
    else:
        norm = jnp.sqrt(jnp.sum(embeddings * embeddings, axis=1, keepdims=True) + 1e-06)
        unit = (embeddings / norm).astype(jnp.bfloat16)
        owner = lax.shift_right_logical(labels, CPO.bit_length() - 1)
        local = jnp.bitwise_and(labels, CPO - 1)
        onehot = (owner[:, None] == jnp.arange(groups, dtype=jnp.int32)[None, :]).astype(jnp.int32)
        rank = jnp.sum(jnp.cumsum(onehot, axis=0) * onehot, axis=1) - 1
        slot = owner * chunk + rank
        place = slot[None, :] == jnp.arange(slots, dtype=jnp.int32)[:, None]
        outgoing = jnp.dot(place.astype(jnp.bfloat16), unit, preferred_element_type=jnp.float32)
        outgoing = outgoing.astype(jnp.bfloat16).reshape(groups, chunk, width)
        tag = jnp.sum(jnp.where(place, local[None, :] + 1, 0), axis=1) - 1
        tag_row = jnp.pad(tag.reshape(groups, chunk), ((0, 0), (0, width - chunk)), constant_values=-1)
        row_id = jnp.arange(chunk, dtype=jnp.int32)
        outgoing = jnp.where(
            (row_id == capacity)[None, :, None], tag_row.astype(jnp.bfloat16)[:, None, :], outgoing
        )
    block = lax.all_to_all(outgoing, "dp", split_axis=0, concat_axis=0, tiled=True)
    top = peers // 2
    far = lax.ppermute(block, "pair", [(p, p ^ top) for p in range(peers)]) if top else None
    left = block.reshape(slots, width)
    left_labels = chunk_labels(block, capacity, chunk)

    def spread(x):
        pieces = [x]
        bit = top // 2
        while bit >= 1:
            perm = [(p, p ^ bit) for p in range(peers)]
            pieces = pieces + [lax.ppermute(y, "pair", perm) for y in pieces]
            bit //= 2
        return pieces

    def best_over(pieces, first_is_own):
        best = None
        for index, piece in enumerate(pieces):
            piece_max = piece_best(
                left,
                left_labels,
                piece.reshape(slots, width),
                chunk_labels(piece, capacity, chunk),
                first_is_own and index == 0,
            )
            best = piece_max if best is None else jnp.maximum(best, piece_max)
        return best

    best = best_over(spread(block), True)
    if far is not None:
        far, best = lax.optimization_barrier((far, best))
        best = jnp.maximum(best, best_over(spread(far), False))
    lanes = -(-chunk // 128) * 128
    sent = jnp.pad(best.reshape(groups, 1, chunk), ((0, 0), (0, 7), (0, lanes - chunk)))
    returned = lax.all_to_all(sent, "dp", split_axis=0, concat_axis=0, tiled=True)
    returned = returned[:, 0, :chunk].reshape(slots)
    return jnp.sum(jnp.where(place, returned[:, None], 0.0), axis=0)


def solution(mesh):
    in_specs = (P(("dp", "pair"), None), P(("dp", "pair")))
    out_specs = P(("dp", "pair"))
    return jax.shard_map(shards, mesh=mesh, in_specs=in_specs, out_specs=out_specs, check_vma=False)
```

```python
import functools

import jax
import jax.numpy as jnp
from jax import lax
from jax.experimental import pallas as pl
from jax.experimental.pallas import tpu as pltpu
from jax.sharding import PartitionSpec as P

CPO = 4


floor_value = -2.0


def piece_best(left, left_labels, right, right_labels, exclude_self):
    score = jnp.einsum("id,jd->ij", left, right, preferred_element_type=jnp.float32)
    same = (left_labels[:, None] == right_labels[None, :]) & (left_labels[:, None] >= 0)
    if exclude_self:
        lane = jnp.arange(left.shape[0], dtype=jnp.int32)
        same = same & (lane[:, None] != lane[None, :])
    return jnp.max(jnp.where(same, score, floor_value), axis=1)


def chunk_labels(block, capacity, chunk):
    groups = block.shape[0]
    return block[:, capacity, :chunk].astype(jnp.int32).reshape(groups * chunk)


def prepare_kernel(emb_ref, lrow_ref, out_ref, slot_ref, *, groups, chunk, capacity):
    rows, width = emb_ref.shape
    slots = groups * chunk
    shift = CPO.bit_length() - 1
    e = emb_ref[...]
    norm = jnp.sqrt(jnp.sum(e * e, axis=1, keepdims=True) + 1e-06)
    unit = (e * (1.0 / norm)).astype(jnp.bfloat16)
    lrow = lrow_ref[...]
    orow = lax.shift_right_logical(lrow, shift)
    local_row = jnp.bitwise_and(lrow, CPO - 1)
    first = lax.broadcasted_iota(jnp.int32, (rows, rows), 0)
    second = lax.broadcasted_iota(jnp.int32, (rows, rows), 1)
    ocol = jnp.sum(jnp.where(first == second, orow, 0), axis=1, keepdims=True)
    same = ocol == orow
    rank_row = jnp.sum(jnp.where(same & (first < second), 1, 0), axis=0, keepdims=True)
    rank_col = jnp.sum(jnp.where(same & (second < first), 1, 0), axis=1, keepdims=True)
    slot_row = orow * chunk + rank_row
    slot_ref[...] = slot_row
    place = (lax.broadcasted_iota(jnp.int32, (slots, rows), 0) == slot_row).astype(jnp.bfloat16)
    placed = jnp.dot(place, unit, preferred_element_type=jnp.float32)
    weight = jnp.where(
        lax.broadcasted_iota(jnp.int32, (groups, rows), 0) == orow, local_row + 1, 0
    ).astype(jnp.bfloat16)
    at_rank = (lax.broadcasted_iota(jnp.int32, (rows, width), 1) == rank_col).astype(jnp.bfloat16)
    tags = (jnp.dot(weight, at_rank, preferred_element_type=jnp.float32) - 1.0).astype(jnp.bfloat16)
    out_ref[...] = placed.astype(jnp.bfloat16)
    for g in range(groups):
        out_ref[pl.ds(g * chunk + capacity, 1), :] = tags[g:g + 1, :]


def prepare(embeddings, labels, groups, chunk, capacity):
    rows, width = embeddings.shape
    slots = groups * chunk
    vmem = pltpu.MemorySpace.VMEM
    return pl.pallas_call(
        functools.partial(prepare_kernel, groups=groups, chunk=chunk, capacity=capacity),
        out_shape=(
            jax.ShapeDtypeStruct((slots, width), jnp.bfloat16),
            jax.ShapeDtypeStruct((1, rows), jnp.int32),
        ),
        in_specs=[pl.BlockSpec(memory_space=vmem)] * 2,
        out_specs=(pl.BlockSpec(memory_space=vmem), pl.BlockSpec(memory_space=vmem)),
        cost_estimate=pl.CostEstimate(
            flops=2 * slots * rows * width + 4 * rows * width,
            transcendentals=rows,
            bytes_accessed=rows * width * 4 + slots * width * 2,
        ),
    )(embeddings, labels[None, :])


def shards(embeddings, labels):
    rows, width = embeddings.shape
    groups = lax.axis_size("dp")
    peers = lax.axis_size("pair")
    capacity = 5 * rows // (2 * groups)
    chunk = -(-(capacity + 1) // 16) * 16
    slots = groups * chunk
    if groups <= 16:
        outgoing, slot = prepare(embeddings, labels, groups, chunk, capacity)
        outgoing = outgoing.reshape(groups, chunk, width)
        slot = slot.reshape(rows)
        place = slot[None, :] == jnp.arange(slots, dtype=jnp.int32)[:, None]
    else:
        norm = jnp.sqrt(jnp.sum(embeddings * embeddings, axis=1, keepdims=True) + 1e-06)
        unit = (embeddings / norm).astype(jnp.bfloat16)
        owner = lax.shift_right_logical(labels, CPO.bit_length() - 1)
        local = jnp.bitwise_and(labels, CPO - 1)
        onehot = (owner[:, None] == jnp.arange(groups, dtype=jnp.int32)[None, :]).astype(jnp.int32)
        rank = jnp.sum(jnp.cumsum(onehot, axis=0) * onehot, axis=1) - 1
        slot = owner * chunk + rank
        place = slot[None, :] == jnp.arange(slots, dtype=jnp.int32)[:, None]
        outgoing = jnp.dot(place.astype(jnp.bfloat16), unit, preferred_element_type=jnp.float32)
        outgoing = outgoing.astype(jnp.bfloat16).reshape(groups, chunk, width)
        tag = jnp.sum(jnp.where(place, local[None, :] + 1, 0), axis=1) - 1
        tag_row = jnp.pad(tag.reshape(groups, chunk), ((0, 0), (0, width - chunk)), constant_values=-1)
        row_id = jnp.arange(chunk, dtype=jnp.int32)
        outgoing = jnp.where(
            (row_id == capacity)[None, :, None], tag_row.astype(jnp.bfloat16)[:, None, :], outgoing
        )
    block = lax.all_to_all(outgoing, "dp", split_axis=0, concat_axis=0, tiled=True)
    top = peers // 2
    left = block.reshape(slots, width)
    left_labels = chunk_labels(block, capacity, chunk)
    lanes = -(-chunk // 128) * 128
    far = None
    if top:
        compact = (
            block[:, :capacity, :].reshape(groups * capacity, width),
            block[:, capacity, :lanes],
        )
        far = lax.ppermute(compact, "pair", [(p, p ^ top) for p in range(peers)])

    def spread(x):
        pieces = [x]
        bit = top // 2
        while bit >= 1:
            perm = [(p, p ^ bit) for p in range(peers)]
            pieces = pieces + [lax.ppermute(y, "pair", perm) for y in pieces]
            bit //= 2
        return pieces

    def best_over(pieces, first_is_own):
        best = None
        for index, piece in enumerate(pieces):
            if first_is_own:
                right = piece.reshape(slots, width)
                right_labels = chunk_labels(piece, capacity, chunk)
            else:
                right = piece[0]
                right_labels = piece[1][:, :capacity].astype(jnp.int32).reshape(groups * capacity)
            piece_max = piece_best(
                left, left_labels, right, right_labels, first_is_own and index == 0
            )
            best = piece_max if best is None else jnp.maximum(best, piece_max)
        return best

    best = best_over(spread(block), True)
    if far is not None:
        far, best = lax.optimization_barrier((far, best))
        best = jnp.maximum(best, best_over(spread(far), False))
    sent = jnp.pad(best.reshape(groups, 1, chunk), ((0, 0), (0, 7), (0, lanes - chunk)))
    returned = lax.all_to_all(sent, "dp", split_axis=0, concat_axis=0, tiled=True)
    returned = returned[:, 0, :chunk].reshape(slots)
    return jnp.sum(jnp.where(place, returned[:, None], 0.0), axis=0)


def solution(mesh):
    in_specs = (P(("dp", "pair"), None), P(("dp", "pair")))
    out_specs = P(("dp", "pair"))
    return jax.shard_map(shards, mesh=mesh, in_specs=in_specs, out_specs=out_specs, check_vma=False)
```

```python
import functools

import jax
import jax.numpy as jnp
from jax import lax
from jax.experimental import pallas as pl
from jax.experimental.pallas import tpu as pltpu
from jax.sharding import PartitionSpec as P

CPO = 4


floor_value = -2.0


def piece_best(left, left_labels, right, right_labels, exclude_self):
    score = jnp.einsum("id,jd->ij", left, right, preferred_element_type=jnp.float32)
    same = (left_labels[:, None] == right_labels[None, :]) & (left_labels[:, None] >= 0)
    if exclude_self:
        lane = jnp.arange(left.shape[0], dtype=jnp.int32)
        same = same & (lane[:, None] != lane[None, :])
    return jnp.max(jnp.where(same, score, floor_value), axis=1)


def chunk_labels(block, capacity, chunk):
    groups = block.shape[0]
    return block[:, capacity, :chunk].astype(jnp.int32).reshape(groups * chunk)


def prepare_kernel(emb_ref, lrow_ref, out_ref, slot_ref, *, groups, chunk, capacity):
    rows, width = emb_ref.shape
    slots = groups * chunk
    shift = CPO.bit_length() - 1
    e = emb_ref[...]
    norm = jnp.sqrt(jnp.sum(e * e, axis=1, keepdims=True) + 1e-06)
    unit = (e * (1.0 / norm)).astype(jnp.bfloat16)
    lrow = lrow_ref[...]
    orow = lax.shift_right_logical(lrow, shift)
    local_row = jnp.bitwise_and(lrow, CPO - 1)
    first = lax.broadcasted_iota(jnp.int32, (rows, rows), 0)
    second = lax.broadcasted_iota(jnp.int32, (rows, rows), 1)
    ocol = jnp.sum(jnp.where(first == second, orow, 0), axis=1, keepdims=True)
    same = ocol == orow
    rank_row = jnp.sum(jnp.where(same & (first < second), 1, 0), axis=0, keepdims=True)
    rank_col = jnp.sum(jnp.where(same & (second < first), 1, 0), axis=1, keepdims=True)
    slot_row = orow * chunk + rank_row
    slot_ref[...] = slot_row
    place = (lax.broadcasted_iota(jnp.int32, (slots, rows), 0) == slot_row).astype(jnp.bfloat16)
    placed = jnp.dot(place, unit, preferred_element_type=jnp.float32)
    weight = jnp.where(
        lax.broadcasted_iota(jnp.int32, (groups, rows), 0) == orow, local_row + 1, 0
    ).astype(jnp.bfloat16)
    at_rank = (lax.broadcasted_iota(jnp.int32, (rows, width), 1) == rank_col).astype(jnp.bfloat16)
    tags = (jnp.dot(weight, at_rank, preferred_element_type=jnp.float32) - 1.0).astype(jnp.bfloat16)
    out_ref[...] = placed.astype(jnp.bfloat16)
    for g in range(groups):
        out_ref[pl.ds(g * chunk + capacity, 1), :] = tags[g:g + 1, :]


def prepare(embeddings, labels, groups, chunk, capacity):
    rows, width = embeddings.shape
    slots = groups * chunk
    vmem = pltpu.MemorySpace.VMEM
    return pl.pallas_call(
        functools.partial(prepare_kernel, groups=groups, chunk=chunk, capacity=capacity),
        out_shape=(
            jax.ShapeDtypeStruct((slots, width), jnp.bfloat16),
            jax.ShapeDtypeStruct((1, rows), jnp.int32),
        ),
        in_specs=[pl.BlockSpec(memory_space=vmem)] * 2,
        out_specs=(pl.BlockSpec(memory_space=vmem), pl.BlockSpec(memory_space=vmem)),
        cost_estimate=pl.CostEstimate(
            flops=2 * slots * rows * width + 4 * rows * width,
            transcendentals=rows,
            bytes_accessed=rows * width * 4 + slots * width * 2,
        ),
    )(embeddings, labels[None, :])


def shards(embeddings, labels):
    rows, width = embeddings.shape
    groups = lax.axis_size("dp")
    peers = lax.axis_size("pair")
    capacity = 5 * rows // (2 * groups)
    chunk = -(-(capacity + 1) // 16) * 16
    slots = groups * chunk
    if groups <= 16:
        outgoing, slot = prepare(embeddings, labels, groups, chunk, capacity)
        outgoing = outgoing.reshape(groups, chunk, width)
        slot = slot.reshape(rows)
        place = slot[None, :] == jnp.arange(slots, dtype=jnp.int32)[:, None]
    else:
        norm = jnp.sqrt(jnp.sum(embeddings * embeddings, axis=1, keepdims=True) + 1e-06)
        unit = (embeddings / norm).astype(jnp.bfloat16)
        owner = lax.shift_right_logical(labels, CPO.bit_length() - 1)
        local = jnp.bitwise_and(labels, CPO - 1)
        onehot = (owner[:, None] == jnp.arange(groups, dtype=jnp.int32)[None, :]).astype(jnp.int32)
        rank = jnp.sum(jnp.cumsum(onehot, axis=0) * onehot, axis=1) - 1
        slot = owner * chunk + rank
        place = slot[None, :] == jnp.arange(slots, dtype=jnp.int32)[:, None]
        outgoing = jnp.dot(place.astype(jnp.bfloat16), unit, preferred_element_type=jnp.float32)
        outgoing = outgoing.astype(jnp.bfloat16).reshape(groups, chunk, width)
        tag = jnp.sum(jnp.where(place, local[None, :] + 1, 0), axis=1) - 1
        tag_row = jnp.pad(tag.reshape(groups, chunk), ((0, 0), (0, width - chunk)), constant_values=-1)
        row_id = jnp.arange(chunk, dtype=jnp.int32)
        outgoing = jnp.where(
            (row_id == capacity)[None, :, None], tag_row.astype(jnp.bfloat16)[:, None, :], outgoing
        )
    top = peers // 2
    lanes = -(-chunk // 128) * 128
    me = lax.axis_index("dp")
    pair_perm = [(p, p ^ top) for p in range(peers)]
    early = None
    if top:
        own = lax.dynamic_index_in_dim(outgoing, me, axis=0, keepdims=False)
        early = lax.ppermute((own[:capacity], own[capacity:capacity + 1, :lanes]), "pair", pair_perm)
    block = lax.all_to_all(outgoing, "dp", split_axis=0, concat_axis=0, tiled=True)
    left = block.reshape(slots, width)
    left_labels = chunk_labels(block, capacity, chunk)
    late = None
    if top:
        others = (me + 1 + jnp.arange(groups - 1, dtype=jnp.int32)) % groups
        rest = block[others]
        late = (
            rest[:, :capacity, :].reshape((groups - 1) * capacity, width),
            rest[:, capacity, :lanes],
        )
        late = lax.ppermute(late, "pair", pair_perm)

    def spread(x):
        pieces = [x]
        bit = top // 2
        while bit >= 1:
            perm = [(p, p ^ bit) for p in range(peers)]
            pieces = pieces + [lax.ppermute(y, "pair", perm) for y in pieces]
            bit //= 2
        return pieces

    def best_over(pieces, first_is_own):
        best = None
        for index, piece in enumerate(pieces):
            if first_is_own:
                right = piece.reshape(slots, width)
                right_labels = chunk_labels(piece, capacity, chunk)
            else:
                right = piece[0]
                right_labels = piece[1][:, :capacity].astype(jnp.int32).reshape(right.shape[0])
            piece_max = piece_best(
                left, left_labels, right, right_labels, first_is_own and index == 0
            )
            best = piece_max if best is None else jnp.maximum(best, piece_max)
        return best

    best = best_over(spread(block), True)
    if top:
        best = jnp.maximum(best, best_over(spread(early), False))
        late, best = lax.optimization_barrier((late, best))
        best = jnp.maximum(best, best_over(spread(late), False))
    sent = jnp.pad(best.reshape(groups, 1, chunk), ((0, 0), (0, 7), (0, lanes - chunk)))
    returned = lax.all_to_all(sent, "dp", split_axis=0, concat_axis=0, tiled=True)
    returned = returned[:, 0, :chunk].reshape(slots)
    return jnp.sum(jnp.where(place, returned[:, None], 0.0), axis=0)


def solution(mesh):
    in_specs = (P(("dp", "pair"), None), P(("dp", "pair")))
    out_specs = P(("dp", "pair"))
    return jax.shard_map(shards, mesh=mesh, in_specs=in_specs, out_specs=out_specs, check_vma=False)
```

```python
import functools

import jax
import jax.numpy as jnp
from jax import lax
from jax.experimental import pallas as pl
from jax.experimental.pallas import tpu as pltpu
from jax.sharding import PartitionSpec as P

CPO = 4


floor_value = -2.0


def piece_best(left, left_labels, right, right_labels, exclude_self):
    score = jnp.einsum("id,jd->ij", left, right, preferred_element_type=jnp.float32)
    same = (left_labels[:, None] == right_labels[None, :]) & (left_labels[:, None] >= 0)
    if exclude_self:
        lane = jnp.arange(left.shape[0], dtype=jnp.int32)
        same = same & (lane[:, None] != lane[None, :])
    return jnp.max(jnp.where(same, score, floor_value), axis=1)


def prepare_kernel(emb_ref, lrow_ref, out_ref, slot_ref, *, groups, capacity):
    rows, width = emb_ref.shape
    slots = groups * capacity
    shift = CPO.bit_length() - 1
    e = emb_ref[...]
    norm = jnp.sqrt(jnp.sum(e * e, axis=1, keepdims=True) + 1e-06)
    unit = (e * (1.0 / norm)).astype(jnp.bfloat16)
    lrow = lrow_ref[...]
    orow = lax.shift_right_logical(lrow, shift)
    first = lax.broadcasted_iota(jnp.int32, (rows, rows), 0)
    second = lax.broadcasted_iota(jnp.int32, (rows, rows), 1)
    diagonal = first == second
    ocol = jnp.sum(jnp.where(diagonal, orow, 0), axis=1, keepdims=True)
    lcol = jnp.sum(jnp.where(diagonal, lrow, 0), axis=1, keepdims=True)
    same = ocol == orow
    rank_row = jnp.sum(jnp.where(same & (first < second), 1, 0), axis=0, keepdims=True)
    slot_row = orow * capacity + rank_row
    slot_ref[...] = slot_row
    place = (lax.broadcasted_iota(jnp.int32, (slots, rows), 0) == slot_row).astype(jnp.bfloat16)
    out_ref[:, :width] = jnp.dot(place, unit, preferred_element_type=jnp.float32).astype(jnp.bfloat16)
    tag_source = jnp.where(
        lax.broadcasted_iota(jnp.int32, (rows, 128), 1) == 0, jnp.bitwise_and(lcol, CPO - 1) + 1, 0
    ).astype(jnp.bfloat16)
    tags = jnp.dot(place, tag_source, preferred_element_type=jnp.float32) - 1.0
    out_ref[:, width:] = tags.astype(jnp.bfloat16)


def prepare(embeddings, labels, groups, capacity):
    rows, width = embeddings.shape
    slots = groups * capacity
    vmem = pltpu.MemorySpace.VMEM
    return pl.pallas_call(
        functools.partial(prepare_kernel, groups=groups, capacity=capacity),
        out_shape=(
            jax.ShapeDtypeStruct((slots, width + 128), jnp.bfloat16),
            jax.ShapeDtypeStruct((1, rows), jnp.int32),
        ),
        in_specs=[pl.BlockSpec(memory_space=vmem)] * 2,
        out_specs=(pl.BlockSpec(memory_space=vmem), pl.BlockSpec(memory_space=vmem)),
        cost_estimate=pl.CostEstimate(
            flops=2 * slots * rows * (width + 128) + 4 * rows * width,
            transcendentals=rows,
            bytes_accessed=rows * width * 4 + slots * (width + 128) * 2,
        ),
    )(embeddings, labels[None, :])


def shards(embeddings, labels):
    rows, width = embeddings.shape
    groups = lax.axis_size("dp")
    peers = lax.axis_size("pair")
    capacity = 5 * rows // (2 * groups)
    slots = groups * capacity
    if groups <= 16:
        outgoing, slot = prepare(embeddings, labels, groups, capacity)
        slot = slot.reshape(rows)
    else:
        norm = jnp.sqrt(jnp.sum(embeddings * embeddings, axis=1, keepdims=True) + 1e-06)
        unit = (embeddings / norm).astype(jnp.bfloat16)
        owner = lax.shift_right_logical(labels, CPO.bit_length() - 1)
        local = jnp.bitwise_and(labels, CPO - 1)
        onehot = (owner[:, None] == jnp.arange(groups, dtype=jnp.int32)[None, :]).astype(jnp.int32)
        rank = jnp.sum(jnp.cumsum(onehot, axis=0) * onehot, axis=1) - 1
        slot = owner * capacity + rank
        tag_source = jnp.zeros((rows, 128), jnp.bfloat16).at[:, 0].set((local + 1).astype(jnp.bfloat16))
        source = jnp.concatenate([unit, tag_source], axis=1)
        place = slot[None, :] == jnp.arange(slots, dtype=jnp.int32)[:, None]
        outgoing = jnp.dot(place.astype(jnp.bfloat16), source, preferred_element_type=jnp.float32)
        outgoing = (outgoing - jnp.where(jnp.arange(width + 128) >= width, 1.0, 0.0)).astype(jnp.bfloat16)
    place = slot[None, :] == jnp.arange(slots, dtype=jnp.int32)[:, None]
    outgoing = outgoing.reshape(groups, capacity, width + 128)
    block = lax.all_to_all(outgoing, "dp", split_axis=0, concat_axis=0, tiled=True)
    block = block.reshape(slots, width + 128)
    top = peers // 2
    own = (block[:, :width], block[:, width])
    far = lax.ppermute(own, "pair", [(p, p ^ top) for p in range(peers)]) if top else None

    def spread(x):
        pieces = [x]
        bit = top // 2
        while bit >= 1:
            perm = [(p, p ^ bit) for p in range(peers)]
            pieces = pieces + [lax.ppermute(y, "pair", perm) for y in pieces]
            bit //= 2
        return pieces

    left, left_tags = own
    left_labels = left_tags.astype(jnp.int32)

    def best_over(pieces, first_is_own):
        best = None
        for index, (right, right_tags) in enumerate(pieces):
            piece_max = piece_best(
                left, left_labels, right, right_tags.astype(jnp.int32), first_is_own and index == 0
            )
            best = piece_max if best is None else jnp.maximum(best, piece_max)
        return best

    best = best_over(spread(own), True)
    if far is not None:
        far, best = lax.optimization_barrier((far, best))
        best = jnp.maximum(best, best_over(spread(far), False))
    lanes = -(-capacity // 128) * 128
    sent = jnp.pad(best.reshape(groups, 1, capacity), ((0, 0), (0, 7), (0, lanes - capacity)))
    returned = lax.all_to_all(sent, "dp", split_axis=0, concat_axis=0, tiled=True)
    returned = returned[:, 0, :capacity].reshape(slots)
    return jnp.sum(jnp.where(place, returned[:, None], 0.0), axis=0)


def solution(mesh):
    in_specs = (P(("dp", "pair"), None), P(("dp", "pair")))
    out_specs = P(("dp", "pair"))
    return jax.shard_map(shards, mesh=mesh, in_specs=in_specs, out_specs=out_specs, check_vma=False)
```

```python
import functools

import jax
import jax.numpy as jnp
from jax import lax
from jax.experimental import pallas as pl
from jax.experimental.pallas import tpu as pltpu
from jax.sharding import PartitionSpec as P

CPO = 4
TAG_LANES = 16


floor_value = -2.0


def piece_best(left, left_labels, right, right_labels, exclude_self):
    score = jnp.einsum("id,jd->ij", left, right, preferred_element_type=jnp.float32)
    same = (left_labels[:, None] == right_labels[None, :]) & (left_labels[:, None] >= 0)
    if exclude_self:
        lane = jnp.arange(left.shape[0], dtype=jnp.int32)
        same = same & (lane[:, None] != lane[None, :])
    return jnp.max(jnp.where(same, score, floor_value), axis=1)


def prepare_kernel(emb_ref, lrow_ref, out_ref, slot_ref, *, groups, capacity):
    rows, width = emb_ref.shape
    slots = groups * capacity
    shift = CPO.bit_length() - 1
    e = emb_ref[...]
    norm = jnp.sqrt(jnp.sum(e * e, axis=1, keepdims=True) + 1e-06)
    unit = (e * (1.0 / norm)).astype(jnp.bfloat16)
    lrow = lrow_ref[...]
    orow = lax.shift_right_logical(lrow, shift)
    first = lax.broadcasted_iota(jnp.int32, (rows, rows), 0)
    second = lax.broadcasted_iota(jnp.int32, (rows, rows), 1)
    diagonal = first == second
    ocol = jnp.sum(jnp.where(diagonal, orow, 0), axis=1, keepdims=True)
    lcol = jnp.sum(jnp.where(diagonal, lrow, 0), axis=1, keepdims=True)
    same = ocol == orow
    rank_row = jnp.sum(jnp.where(same & (first < second), 1, 0), axis=0, keepdims=True)
    slot_row = orow * capacity + rank_row
    slot_ref[...] = slot_row
    place = (lax.broadcasted_iota(jnp.int32, (slots, rows), 0) == slot_row).astype(jnp.bfloat16)
    out_ref[:, :width] = jnp.dot(place, unit, preferred_element_type=jnp.float32).astype(jnp.bfloat16)
    tag_source = jnp.where(
        lax.broadcasted_iota(jnp.int32, (rows, TAG_LANES), 1) == 0, jnp.bitwise_and(lcol, CPO - 1) + 1, 0
    ).astype(jnp.bfloat16)
    tags = jnp.dot(place, tag_source, preferred_element_type=jnp.float32) - 1.0
    out_ref[:, width:] = tags.astype(jnp.bfloat16)


def prepare(embeddings, labels, groups, capacity):
    rows, width = embeddings.shape
    slots = groups * capacity
    vmem = pltpu.MemorySpace.VMEM
    return pl.pallas_call(
        functools.partial(prepare_kernel, groups=groups, capacity=capacity),
        out_shape=(
            jax.ShapeDtypeStruct((slots, width + TAG_LANES), jnp.bfloat16),
            jax.ShapeDtypeStruct((1, rows), jnp.int32),
        ),
        in_specs=[pl.BlockSpec(memory_space=vmem)] * 2,
        out_specs=(pl.BlockSpec(memory_space=vmem), pl.BlockSpec(memory_space=vmem)),
        cost_estimate=pl.CostEstimate(
            flops=2 * slots * rows * (width + TAG_LANES) + 4 * rows * width,
            transcendentals=rows,
            bytes_accessed=rows * width * 4 + slots * (width + TAG_LANES) * 2,
        ),
    )(embeddings, labels[None, :])


def shards(embeddings, labels):
    rows, width = embeddings.shape
    groups = lax.axis_size("dp")
    peers = lax.axis_size("pair")
    capacity = 5 * rows // (2 * groups)
    slots = groups * capacity
    if groups <= 16:
        outgoing, slot = prepare(embeddings, labels, groups, capacity)
        slot = slot.reshape(rows)
    else:
        norm = jnp.sqrt(jnp.sum(embeddings * embeddings, axis=1, keepdims=True) + 1e-06)
        unit = (embeddings / norm).astype(jnp.bfloat16)
        owner = lax.shift_right_logical(labels, CPO.bit_length() - 1)
        local = jnp.bitwise_and(labels, CPO - 1)
        onehot = (owner[:, None] == jnp.arange(groups, dtype=jnp.int32)[None, :]).astype(jnp.int32)
        rank = jnp.sum(jnp.cumsum(onehot, axis=0) * onehot, axis=1) - 1
        slot = owner * capacity + rank
        tag_source = jnp.zeros((rows, TAG_LANES), jnp.bfloat16).at[:, 0].set((local + 1).astype(jnp.bfloat16))
        source = jnp.concatenate([unit, tag_source], axis=1)
        place = slot[None, :] == jnp.arange(slots, dtype=jnp.int32)[:, None]
        outgoing = jnp.dot(place.astype(jnp.bfloat16), source, preferred_element_type=jnp.float32)
        outgoing = (outgoing - jnp.where(jnp.arange(width + TAG_LANES) >= width, 1.0, 0.0)).astype(jnp.bfloat16)
    place = slot[None, :] == jnp.arange(slots, dtype=jnp.int32)[:, None]
    outgoing = outgoing.reshape(groups, capacity, width + TAG_LANES)
    block = lax.all_to_all(outgoing, "dp", split_axis=0, concat_axis=0, tiled=True)
    block = block.reshape(slots, width + TAG_LANES)
    top = peers // 2
    own = (block[:, :width], block[:, width])
    far = lax.ppermute(own, "pair", [(p, p ^ top) for p in range(peers)]) if top else None

    def spread(x):
        pieces = [x]
        bit = top // 2
        while bit >= 1:
            perm = [(p, p ^ bit) for p in range(peers)]
            pieces = pieces + [lax.ppermute(y, "pair", perm) for y in pieces]
            bit //= 2
        return pieces

    left, left_tags = own
    left_labels = left_tags.astype(jnp.int32)

    def best_over(pieces, first_is_own):
        best = None
        for index, (right, right_tags) in enumerate(pieces):
            piece_max = piece_best(
                left, left_labels, right, right_tags.astype(jnp.int32), first_is_own and index == 0
            )
            best = piece_max if best is None else jnp.maximum(best, piece_max)
        return best

    best = best_over(spread(own), True)
    if far is not None:
        far, best = lax.optimization_barrier((far, best))
        best = jnp.maximum(best, best_over(spread(far), False))
    lanes = -(-capacity // 128) * 128
    sent = jnp.pad(best.reshape(groups, 1, capacity), ((0, 0), (0, 7), (0, lanes - capacity)))
    returned = lax.all_to_all(sent, "dp", split_axis=0, concat_axis=0, tiled=True)
    returned = returned[:, 0, :capacity].reshape(slots)
    return jnp.sum(jnp.where(place, returned[:, None], 0.0), axis=0)


def solution(mesh):
    in_specs = (P(("dp", "pair"), None), P(("dp", "pair")))
    out_specs = P(("dp", "pair"))
    return jax.shard_map(shards, mesh=mesh, in_specs=in_specs, out_specs=out_specs, check_vma=False)
```

```python
import functools

import jax
import jax.numpy as jnp
from jax import lax
from jax.experimental import pallas as pl
from jax.experimental.pallas import tpu as pltpu
from jax.sharding import PartitionSpec as P

CPO = 4


floor_value = -2.0


def piece_best(left, left_labels, right, right_labels, exclude_self):
    score = jnp.einsum("id,jd->ij", left, right, preferred_element_type=jnp.float32)
    same = (left_labels[:, None] == right_labels[None, :]) & (left_labels[:, None] >= 0)
    if exclude_self:
        lane = jnp.arange(left.shape[0], dtype=jnp.int32)
        same = same & (lane[:, None] != lane[None, :])
    return jnp.max(jnp.where(same, score, floor_value), axis=1)


def prepare_kernel(emb_ref, lrow_ref, out_ref, slot_ref, *, groups, capacity):
    rows, width = emb_ref.shape
    slots = groups * capacity
    shift = CPO.bit_length() - 1
    e = emb_ref[...]
    norm = jnp.sqrt(jnp.sum(e * e, axis=1, keepdims=True) + 1e-06)
    unit = (e * (1.0 / norm)).astype(jnp.bfloat16)
    lrow = lrow_ref[...]
    orow = lax.shift_right_logical(lrow, shift)
    first = lax.broadcasted_iota(jnp.int32, (rows, rows), 0)
    second = lax.broadcasted_iota(jnp.int32, (rows, rows), 1)
    diagonal = first == second
    ocol = jnp.sum(jnp.where(diagonal, orow, 0), axis=1, keepdims=True)
    lcol = jnp.sum(jnp.where(diagonal, lrow, 0), axis=1, keepdims=True)
    same = ocol == orow
    rank_row = jnp.sum(jnp.where(same & (first < second), 1, 0), axis=0, keepdims=True)
    slot_row = orow * capacity + rank_row
    slot_ref[...] = slot_row
    place = (lax.broadcasted_iota(jnp.int32, (slots, rows), 0) == slot_row).astype(jnp.bfloat16)
    out_ref[:, :width] = jnp.dot(place, unit, preferred_element_type=jnp.float32).astype(jnp.bfloat16)
    tag_source = jnp.where(
        lax.broadcasted_iota(jnp.int32, (rows, 128), 1) == 0, jnp.bitwise_and(lcol, CPO - 1) + 1, 0
    ).astype(jnp.bfloat16)
    tags = jnp.dot(place, tag_source, preferred_element_type=jnp.float32) - 1.0
    out_ref[:, width:] = tags.astype(jnp.bfloat16)


def prepare(embeddings, labels, groups, capacity):
    rows, width = embeddings.shape
    slots = groups * capacity
    vmem = pltpu.MemorySpace.VMEM
    return pl.pallas_call(
        functools.partial(prepare_kernel, groups=groups, capacity=capacity),
        out_shape=(
            jax.ShapeDtypeStruct((slots, width + 128), jnp.bfloat16),
            jax.ShapeDtypeStruct((1, rows), jnp.int32),
        ),
        in_specs=[pl.BlockSpec(memory_space=vmem)] * 2,
        out_specs=(pl.BlockSpec(memory_space=vmem), pl.BlockSpec(memory_space=vmem)),
        cost_estimate=pl.CostEstimate(
            flops=2 * slots * rows * (width + 128) + 4 * rows * width,
            transcendentals=rows,
            bytes_accessed=rows * width * 4 + slots * (width + 128) * 2,
        ),
    )(embeddings, labels[None, :])


def shards(embeddings, labels):
    rows, width = embeddings.shape
    groups = lax.axis_size("dp")
    peers = lax.axis_size("pair")
    capacity = 5 * rows // (2 * groups)
    slots = groups * capacity
    if groups <= 16:
        outgoing, slot = prepare(embeddings, labels, groups, capacity)
        slot = slot.reshape(rows)
    else:
        norm = jnp.sqrt(jnp.sum(embeddings * embeddings, axis=1, keepdims=True) + 1e-06)
        unit = (embeddings / norm).astype(jnp.bfloat16)
        owner = lax.shift_right_logical(labels, CPO.bit_length() - 1)
        local = jnp.bitwise_and(labels, CPO - 1)
        onehot = (owner[:, None] == jnp.arange(groups, dtype=jnp.int32)[None, :]).astype(jnp.int32)
        rank = jnp.sum(jnp.cumsum(onehot, axis=0) * onehot, axis=1) - 1
        slot = owner * capacity + rank
        tag_source = jnp.zeros((rows, 128), jnp.bfloat16).at[:, 0].set((local + 1).astype(jnp.bfloat16))
        source = jnp.concatenate([unit, tag_source], axis=1)
        place = slot[None, :] == jnp.arange(slots, dtype=jnp.int32)[:, None]
        outgoing = jnp.dot(place.astype(jnp.bfloat16), source, preferred_element_type=jnp.float32)
        outgoing = (outgoing - jnp.where(jnp.arange(width + 128) >= width, 1.0, 0.0)).astype(jnp.bfloat16)
    place = slot[None, :] == jnp.arange(slots, dtype=jnp.int32)[:, None]
    outgoing = outgoing.reshape(groups, capacity, width + 128)
    block = lax.all_to_all(outgoing, "dp", split_axis=0, concat_axis=0, tiled=True)
    block = block.reshape(slots, width + 128)
    top = peers // 2
    own = (block[:, :width], block[:, width])
    far = lax.ppermute(own, "pair", [(p, p ^ top) for p in range(peers)]) if top else None

    def spread(x):
        pieces = [x]
        bit = top // 2
        while bit >= 1:
            perm = [(p, p ^ bit) for p in range(peers)]
            pieces = pieces + [lax.ppermute(y, "pair", perm) for y in pieces]
            bit //= 2
        return pieces

    left, left_tags = own
    left_labels = left_tags.astype(jnp.int32)

    def best_over(pieces, first_is_own):
        best = None
        for index, (right, right_tags) in enumerate(pieces):
            piece_max = piece_best(
                left, left_labels, right, right_tags.astype(jnp.int32), first_is_own and index == 0
            )
            best = piece_max if best is None else jnp.maximum(best, piece_max)
        return best

    best = best_over(spread(own), True)
    if far is not None:
        far, best = lax.optimization_barrier((far, best))
        best = jnp.maximum(best, best_over(spread(far), False))
    place, best = lax.optimization_barrier((place, best))
    lanes = -(-capacity // 128) * 128
    sent = jnp.pad(best.reshape(groups, 1, capacity), ((0, 0), (0, 7), (0, lanes - capacity)))
    returned = lax.all_to_all(sent, "dp", split_axis=0, concat_axis=0, tiled=True)
    returned = returned[:, 0, :capacity].reshape(slots)
    return jnp.sum(jnp.where(place, returned[:, None], 0.0), axis=0)


def solution(mesh):
    in_specs = (P(("dp", "pair"), None), P(("dp", "pair")))
    out_specs = P(("dp", "pair"))
    return jax.shard_map(shards, mesh=mesh, in_specs=in_specs, out_specs=out_specs, check_vma=False)
```

```python
import functools

import jax
import jax.numpy as jnp
from jax import lax
from jax.experimental import pallas as pl
from jax.experimental.pallas import tpu as pltpu
from jax.sharding import PartitionSpec as P

CPO = 4


floor_value = -2.0


def piece_best(left, left_labels, right, right_labels, exclude_self):
    score = jnp.einsum("id,jd->ij", left, right, preferred_element_type=jnp.float32)
    same = (left_labels[:, None] == right_labels[None, :]) & (left_labels[:, None] >= 0)
    if exclude_self:
        lane = jnp.arange(left.shape[0], dtype=jnp.int32)
        same = same & (lane[:, None] != lane[None, :])
    return jnp.max(jnp.where(same, score, floor_value), axis=1)


def prepare_kernel(emb_ref, lrow_ref, out_ref, slot_ref, *, groups, capacity):
    rows, width = emb_ref.shape
    slots = groups * capacity
    shift = CPO.bit_length() - 1
    e = emb_ref[...]
    norm = jnp.sqrt(jnp.sum(e * e, axis=1, keepdims=True) + 1e-06)
    unit = (e * (1.0 / norm)).astype(jnp.bfloat16)
    lrow = lrow_ref[...]
    orow = lax.shift_right_logical(lrow, shift)
    first = lax.broadcasted_iota(jnp.int32, (rows, rows), 0)
    second = lax.broadcasted_iota(jnp.int32, (rows, rows), 1)
    diagonal = first == second
    ocol = jnp.sum(jnp.where(diagonal, orow, 0), axis=1, keepdims=True)
    lcol = jnp.sum(jnp.where(diagonal, lrow, 0), axis=1, keepdims=True)
    same = ocol == orow
    rank_row = jnp.sum(jnp.where(same & (first < second), 1, 0), axis=0, keepdims=True)
    slot_row = orow * capacity + rank_row
    slot_ref[...] = slot_row
    place = (lax.broadcasted_iota(jnp.int32, (slots, rows), 0) == slot_row).astype(jnp.bfloat16)
    out_ref[:, :width] = jnp.dot(place, unit, preferred_element_type=jnp.float32).astype(jnp.bfloat16)
    tag_source = jnp.where(
        lax.broadcasted_iota(jnp.int32, (rows, 128), 1) == 0, jnp.bitwise_and(lcol, CPO - 1) + 1, 0
    ).astype(jnp.bfloat16)
    tags = jnp.dot(place, tag_source, preferred_element_type=jnp.float32) - 1.0
    out_ref[:, width:] = tags.astype(jnp.bfloat16)


def prepare(embeddings, labels, groups, capacity):
    rows, width = embeddings.shape
    slots = groups * capacity
    vmem = pltpu.MemorySpace.VMEM
    return pl.pallas_call(
        functools.partial(prepare_kernel, groups=groups, capacity=capacity),
        out_shape=(
            jax.ShapeDtypeStruct((slots, width + 128), jnp.bfloat16),
            jax.ShapeDtypeStruct((1, rows), jnp.int32),
        ),
        in_specs=[pl.BlockSpec(memory_space=vmem)] * 2,
        out_specs=(pl.BlockSpec(memory_space=vmem), pl.BlockSpec(memory_space=vmem)),
        cost_estimate=pl.CostEstimate(
            flops=2 * slots * rows * (width + 128) + 4 * rows * width,
            transcendentals=rows,
            bytes_accessed=rows * width * 4 + slots * (width + 128) * 2,
        ),
    )(embeddings, labels[None, :])


def shards(embeddings, labels):
    rows, width = embeddings.shape
    groups = lax.axis_size("dp")
    peers = lax.axis_size("pair")
    capacity = 5 * rows // (2 * groups)
    slots = groups * capacity
    if groups <= 16:
        outgoing, slot = prepare(embeddings, labels, groups, capacity)
        slot = slot.reshape(rows)
    else:
        norm = jnp.sqrt(jnp.sum(embeddings * embeddings, axis=1, keepdims=True) + 1e-06)
        unit = (embeddings / norm).astype(jnp.bfloat16)
        owner = lax.shift_right_logical(labels, CPO.bit_length() - 1)
        local = jnp.bitwise_and(labels, CPO - 1)
        onehot = (owner[:, None] == jnp.arange(groups, dtype=jnp.int32)[None, :]).astype(jnp.int32)
        rank = jnp.sum(jnp.cumsum(onehot, axis=0) * onehot, axis=1) - 1
        slot = owner * capacity + rank
        tag_source = jnp.zeros((rows, 128), jnp.bfloat16).at[:, 0].set((local + 1).astype(jnp.bfloat16))
        source = jnp.concatenate([unit, tag_source], axis=1)
        place = slot[None, :] == jnp.arange(slots, dtype=jnp.int32)[:, None]
        outgoing = jnp.dot(place.astype(jnp.bfloat16), source, preferred_element_type=jnp.float32)
        outgoing = (outgoing - jnp.where(jnp.arange(width + 128) >= width, 1.0, 0.0)).astype(jnp.bfloat16)
    place = slot[None, :] == jnp.arange(slots, dtype=jnp.int32)[:, None]
    outgoing = outgoing.reshape(groups, capacity, width + 128)
    block = lax.all_to_all(outgoing, "dp", split_axis=0, concat_axis=0, tiled=True)
    block = block.reshape(slots, width + 128)
    top = peers // 2
    own = (block[:, :width], block[:, width])

    def spread(x):
        pieces = [x]
        bit = top // 2
        while bit >= 1:
            perm = [(p, p ^ bit) for p in range(peers)]
            pieces = pieces + [lax.ppermute(y, "pair", perm) for y in pieces]
            bit //= 2
        return pieces

    masks = [0]
    bit = top // 2
    while bit >= 1:
        masks = masks + [m ^ bit for m in masks]
        bit //= 2
    far = None
    if top:
        far_tags = [
            lax.ppermute(own[1], "pair", [(p, p ^ top ^ m) for p in range(peers)]) for m in masks
        ]
        far_rows = lax.ppermute(own[0], "pair", [(p, p ^ top) for p in range(peers)])
        far = (far_rows, far_tags)

    left, left_tags = own
    left_labels = left_tags.astype(jnp.int32)

    def best_over(pieces, first_is_own):
        best = None
        for index, (right, right_tags) in enumerate(pieces):
            piece_max = piece_best(
                left, left_labels, right, right_tags.astype(jnp.int32), first_is_own and index == 0
            )
            best = piece_max if best is None else jnp.maximum(best, piece_max)
        return best

    best = best_over(spread(own), True)
    if far is not None:
        far, best = lax.optimization_barrier((far, best))
        far_rows, far_tags = far
        best = jnp.maximum(best, best_over(list(zip(spread(far_rows), far_tags)), False))
    place, best = lax.optimization_barrier((place, best))
    lanes = -(-capacity // 128) * 128
    sent = jnp.pad(best.reshape(groups, 1, capacity), ((0, 0), (0, 7), (0, lanes - capacity)))
    returned = lax.all_to_all(sent, "dp", split_axis=0, concat_axis=0, tiled=True)
    returned = returned[:, 0, :capacity].reshape(slots)
    return jnp.sum(jnp.where(place, returned[:, None], 0.0), axis=0)


def solution(mesh):
    in_specs = (P(("dp", "pair"), None), P(("dp", "pair")))
    out_specs = P(("dp", "pair"))
    return jax.shard_map(shards, mesh=mesh, in_specs=in_specs, out_specs=out_specs, check_vma=False)
```

```python
import functools

import jax
import jax.numpy as jnp
from jax import lax
from jax.experimental import pallas as pl
from jax.experimental.pallas import tpu as pltpu
from jax.sharding import PartitionSpec as P

CPO = 4


floor_value = -2.0


def piece_best(left, left_labels, right, right_labels, exclude_self):
    score = jnp.einsum("id,jd->ij", left, right, preferred_element_type=jnp.float32)
    same = (left_labels[:, None] == right_labels[None, :]) & (left_labels[:, None] >= 0)
    if exclude_self:
        lane = jnp.arange(left.shape[0], dtype=jnp.int32)
        same = same & (lane[:, None] != lane[None, :])
    return jnp.max(jnp.where(same, score, floor_value), axis=1)


def prepare_kernel(emb_ref, lrow_ref, out_ref, slot_ref, *, groups, capacity):
    rows, width = emb_ref.shape
    slots = groups * capacity
    shift = CPO.bit_length() - 1
    e = emb_ref[...]
    norm = jnp.sqrt(jnp.sum(e * e, axis=1, keepdims=True) + 1e-06)
    unit = (e * (1.0 / norm)).astype(jnp.bfloat16)
    lrow = lrow_ref[...]
    orow = lax.shift_right_logical(lrow, shift)
    first = lax.broadcasted_iota(jnp.int32, (rows, rows), 0)
    second = lax.broadcasted_iota(jnp.int32, (rows, rows), 1)
    diagonal = first == second
    ocol = jnp.sum(jnp.where(diagonal, orow, 0), axis=1, keepdims=True)
    lcol = jnp.sum(jnp.where(diagonal, lrow, 0), axis=1, keepdims=True)
    same = ocol == orow
    rank_row = jnp.sum(jnp.where(same & (first < second), 1, 0), axis=0, keepdims=True)
    slot_row = orow * capacity + rank_row
    slot_ref[...] = slot_row
    place = (lax.broadcasted_iota(jnp.int32, (slots, rows), 0) == slot_row).astype(jnp.bfloat16)
    out_ref[:, :width] = jnp.dot(place, unit, preferred_element_type=jnp.float32).astype(jnp.bfloat16)
    tag_source = jnp.where(
        lax.broadcasted_iota(jnp.int32, (rows, 128), 1) == 0, jnp.bitwise_and(lcol, CPO - 1) + 1, 0
    ).astype(jnp.bfloat16)
    tags = jnp.dot(place, tag_source, preferred_element_type=jnp.float32) - 1.0
    out_ref[:, width:] = tags.astype(jnp.bfloat16)


def prepare(embeddings, labels, groups, capacity):
    rows, width = embeddings.shape
    slots = groups * capacity
    vmem = pltpu.MemorySpace.VMEM
    return pl.pallas_call(
        functools.partial(prepare_kernel, groups=groups, capacity=capacity),
        out_shape=(
            jax.ShapeDtypeStruct((slots, width + 128), jnp.bfloat16),
            jax.ShapeDtypeStruct((1, rows), jnp.int32),
        ),
        in_specs=[pl.BlockSpec(memory_space=vmem)] * 2,
        out_specs=(pl.BlockSpec(memory_space=vmem), pl.BlockSpec(memory_space=vmem)),
        cost_estimate=pl.CostEstimate(
            flops=2 * slots * rows * (width + 128) + 4 * rows * width,
            transcendentals=rows,
            bytes_accessed=rows * width * 4 + slots * (width + 128) * 2,
        ),
    )(embeddings, labels[None, :])


def shards(embeddings, labels):
    rows, width = embeddings.shape
    groups = lax.axis_size("dp")
    peers = lax.axis_size("pair")
    capacity = 5 * rows // (2 * groups)
    slots = groups * capacity
    if groups <= 16:
        outgoing, slot = prepare(embeddings, labels, groups, capacity)
        slot = slot.reshape(rows)
    else:
        norm = jnp.sqrt(jnp.sum(embeddings * embeddings, axis=1, keepdims=True) + 1e-06)
        unit = (embeddings / norm).astype(jnp.bfloat16)
        owner = lax.shift_right_logical(labels, CPO.bit_length() - 1)
        local = jnp.bitwise_and(labels, CPO - 1)
        onehot = (owner[:, None] == jnp.arange(groups, dtype=jnp.int32)[None, :]).astype(jnp.int32)
        rank = jnp.sum(jnp.cumsum(onehot, axis=0) * onehot, axis=1) - 1
        slot = owner * capacity + rank
        tag_source = jnp.zeros((rows, 128), jnp.bfloat16).at[:, 0].set((local + 1).astype(jnp.bfloat16))
        source = jnp.concatenate([unit, tag_source], axis=1)
        place = slot[None, :] == jnp.arange(slots, dtype=jnp.int32)[:, None]
        outgoing = jnp.dot(place.astype(jnp.bfloat16), source, preferred_element_type=jnp.float32)
        outgoing = (outgoing - jnp.where(jnp.arange(width + 128) >= width, 1.0, 0.0)).astype(jnp.bfloat16)
    place = slot[None, :] == jnp.arange(slots, dtype=jnp.int32)[:, None]
    outgoing = outgoing.reshape(groups, capacity, width + 128)
    block = lax.all_to_all(outgoing, "dp", split_axis=0, concat_axis=0, tiled=True)
    block = block.reshape(slots, width + 128)
    top = peers // 2
    own = (block[:, :width], block[:, width])
    far = lax.ppermute(own, "pair", [(p, p ^ top) for p in range(peers)]) if top else None

    def spread(x):
        pieces, masks = [x], [0]
        bit = top // 2
        while bit >= 1:
            perm = [(p, p ^ bit) for p in range(peers)]
            pieces = pieces + [lax.ppermute(y, "pair", perm) for y in pieces]
            masks = masks + [m ^ bit for m in masks]
            bit //= 2
        return pieces, masks

    left, left_tags = own
    left_labels = left_tags.astype(jnp.int32)
    near, masks = spread(own)
    best = None
    for index, (right, right_tags) in enumerate(near):
        piece_max = piece_best(left, left_labels, right, right_tags.astype(jnp.int32), index == 0)
        best = piece_max if best is None else jnp.maximum(best, piece_max)
    late_labels, best = lax.optimization_barrier((labels, best))
    owner = lax.shift_right_logical(late_labels, CPO.bit_length() - 1)
    onehot = (owner[:, None] == jnp.arange(groups, dtype=jnp.int32)[None, :]).astype(jnp.int32)
    rank = jnp.sum(jnp.cumsum(onehot, axis=0) * onehot, axis=1) - 1
    place = (owner * capacity + rank)[None, :] == jnp.arange(slots, dtype=jnp.int32)[:, None]
    if far is not None:
        far, near, best, place = lax.optimization_barrier((far, near, best, place))
        far_rows, far_tags = far
        far_labels = far_tags.astype(jnp.int32)
        for (rows_j, tags_j), m in zip(near, masks):
            piece_max = piece_best(rows_j, tags_j.astype(jnp.int32), far_rows, far_labels, False)
            if m:
                piece_max = lax.ppermute(piece_max, "pair", [(p, p ^ m) for p in range(peers)])
            best = jnp.maximum(best, piece_max)
    lanes = -(-capacity // 128) * 128
    sent = jnp.pad(best.reshape(groups, 1, capacity), ((0, 0), (0, 7), (0, lanes - capacity)))
    returned = lax.all_to_all(sent, "dp", split_axis=0, concat_axis=0, tiled=True)
    returned = returned[:, 0, :capacity].reshape(slots)
    return jnp.sum(jnp.where(place, returned[:, None], 0.0), axis=0)


def solution(mesh):
    in_specs = (P(("dp", "pair"), None), P(("dp", "pair")))
    out_specs = P(("dp", "pair"))
    return jax.shard_map(shards, mesh=mesh, in_specs=in_specs, out_specs=out_specs, check_vma=False)
```

```python
import functools

import jax
import jax.numpy as jnp
from jax import lax
from jax.experimental import pallas as pl
from jax.experimental.pallas import tpu as pltpu
from jax.sharding import PartitionSpec as P

CPO = 4


floor_value = -2.0


def piece_best(left, left_labels, right, right_labels, exclude_self):
    score = jnp.einsum("id,jd->ij", left, right, preferred_element_type=jnp.float32)
    same = (left_labels[:, None] == right_labels[None, :]) & (left_labels[:, None] >= 0)
    if exclude_self:
        lane = jnp.arange(left.shape[0], dtype=jnp.int32)
        same = same & (lane[:, None] != lane[None, :])
    return jnp.max(jnp.where(same, score, floor_value), axis=1)


def prepare_kernel(emb_ref, lrow_ref, out_ref, slot_ref, *, groups, capacity):
    rows, width = emb_ref.shape
    slots = groups * capacity
    shift = CPO.bit_length() - 1
    e = emb_ref[...]
    norm = jnp.sqrt(jnp.sum(e * e, axis=1, keepdims=True) + 1e-06)
    unit = (e * (1.0 / norm)).astype(jnp.bfloat16)
    lrow = lrow_ref[...]
    orow = lax.shift_right_logical(lrow, shift)
    first = lax.broadcasted_iota(jnp.int32, (rows, rows), 0)
    second = lax.broadcasted_iota(jnp.int32, (rows, rows), 1)
    diagonal = first == second
    ocol = jnp.sum(jnp.where(diagonal, orow, 0), axis=1, keepdims=True)
    lcol = jnp.sum(jnp.where(diagonal, lrow, 0), axis=1, keepdims=True)
    same = ocol == orow
    rank_row = jnp.sum(jnp.where(same & (first < second), 1, 0), axis=0, keepdims=True)
    slot_row = orow * capacity + rank_row
    slot_ref[...] = slot_row
    place = (lax.broadcasted_iota(jnp.int32, (slots, rows), 0) == slot_row).astype(jnp.bfloat16)
    out_ref[:, :width] = jnp.dot(place, unit, preferred_element_type=jnp.float32).astype(jnp.bfloat16)
    tag_lane = lax.broadcasted_iota(jnp.int32, (rows, 128), 1)
    tag_source = jnp.where(
        tag_lane == 0,
        jnp.bitwise_and(lcol, CPO - 1) + 1,
        jnp.where(tag_lane == 1, lax.broadcasted_iota(jnp.int32, (rows, 128), 0) + 1, 0),
    ).astype(jnp.bfloat16)
    tags = jnp.dot(place, tag_source, preferred_element_type=jnp.float32) - 1.0
    out_ref[:, width:] = tags.astype(jnp.bfloat16)


def prepare(embeddings, labels, groups, capacity):
    rows, width = embeddings.shape
    slots = groups * capacity
    vmem = pltpu.MemorySpace.VMEM
    return pl.pallas_call(
        functools.partial(prepare_kernel, groups=groups, capacity=capacity),
        out_shape=(
            jax.ShapeDtypeStruct((slots, width + 128), jnp.bfloat16),
            jax.ShapeDtypeStruct((1, rows), jnp.int32),
        ),
        in_specs=[pl.BlockSpec(memory_space=vmem)] * 2,
        out_specs=(pl.BlockSpec(memory_space=vmem), pl.BlockSpec(memory_space=vmem)),
        cost_estimate=pl.CostEstimate(
            flops=2 * slots * rows * (width + 128) + 4 * rows * width,
            transcendentals=rows,
            bytes_accessed=rows * width * 4 + slots * (width + 128) * 2,
        ),
    )(embeddings, labels[None, :])


def shards(embeddings, labels):
    rows, width = embeddings.shape
    groups = lax.axis_size("dp")
    peers = lax.axis_size("pair")
    capacity = 5 * rows // (2 * groups)
    slots = groups * capacity
    if groups <= 16:
        outgoing, slot = prepare(embeddings, labels, groups, capacity)
        slot = slot.reshape(rows)
    else:
        norm = jnp.sqrt(jnp.sum(embeddings * embeddings, axis=1, keepdims=True) + 1e-06)
        unit = (embeddings / norm).astype(jnp.bfloat16)
        owner = lax.shift_right_logical(labels, CPO.bit_length() - 1)
        local = jnp.bitwise_and(labels, CPO - 1)
        onehot = (owner[:, None] == jnp.arange(groups, dtype=jnp.int32)[None, :]).astype(jnp.int32)
        rank = jnp.sum(jnp.cumsum(onehot, axis=0) * onehot, axis=1) - 1
        slot = owner * capacity + rank
        tag_source = jnp.zeros((rows, 128), jnp.bfloat16).at[:, 0].set((local + 1).astype(jnp.bfloat16))
        tag_source = tag_source.at[:, 1].set((jnp.arange(rows) + 1).astype(jnp.bfloat16))
        source = jnp.concatenate([unit, tag_source], axis=1)
        place = slot[None, :] == jnp.arange(slots, dtype=jnp.int32)[:, None]
        outgoing = jnp.dot(place.astype(jnp.bfloat16), source, preferred_element_type=jnp.float32)
        outgoing = (outgoing - jnp.where(jnp.arange(width + 128) >= width, 1.0, 0.0)).astype(jnp.bfloat16)
    outgoing = outgoing.reshape(groups, capacity, width + 128)
    block = lax.all_to_all(outgoing, "dp", split_axis=0, concat_axis=0, tiled=True)
    block = block.reshape(slots, width + 128)
    top = peers // 2
    own = (block[:, :width], block[:, width])
    source_row = block[:, width + 1].astype(jnp.int32).reshape(groups, capacity)
    far = lax.ppermute(own, "pair", [(p, p ^ top) for p in range(peers)]) if top else None

    def spread(x):
        pieces = [x]
        bit = top // 2
        while bit >= 1:
            perm = [(p, p ^ bit) for p in range(peers)]
            pieces = pieces + [lax.ppermute(y, "pair", perm) for y in pieces]
            bit //= 2
        return pieces

    left, left_tags = own
    left_labels = left_tags.astype(jnp.int32)

    def best_over(pieces, first_is_own):
        best = None
        for index, (right, right_tags) in enumerate(pieces):
            piece_max = piece_best(
                left, left_labels, right, right_tags.astype(jnp.int32), first_is_own and index == 0
            )
            best = piece_max if best is None else jnp.maximum(best, piece_max)
        return best

    best = best_over(spread(own), True)
    if far is not None:
        far, best = lax.optimization_barrier((far, best))
        best = jnp.maximum(best, best_over(spread(far), False))
    at_row = source_row[:, :, None] == jnp.arange(rows, dtype=jnp.int32)[None, None, :]
    by_row = jnp.sum(jnp.where(at_row, best.reshape(groups, capacity, 1), 0.0), axis=1)
    sent = jnp.pad(by_row[:, None, :], ((0, 0), (0, 7), (0, 0)))
    returned = lax.all_to_all(sent, "dp", split_axis=0, concat_axis=0, tiled=True)
    return jnp.sum(returned[:, 0, :], axis=0)


def solution(mesh):
    in_specs = (P(("dp", "pair"), None), P(("dp", "pair")))
    out_specs = P(("dp", "pair"))
    return jax.shard_map(shards, mesh=mesh, in_specs=in_specs, out_specs=out_specs, check_vma=False)
```

```python
import functools

import jax
import jax.numpy as jnp
from jax import lax
from jax.experimental import pallas as pl
from jax.experimental.pallas import tpu as pltpu
from jax.sharding import PartitionSpec as P

CPO = 4


floor_value = -2.0


def piece_best(left, left_labels, right, right_labels, exclude_self):
    score = jnp.einsum("id,jd->ij", left, right, preferred_element_type=jnp.float32)
    same = (left_labels[:, None] == right_labels[None, :]) & (left_labels[:, None] >= 0)
    if exclude_self:
        lane = jnp.arange(left.shape[0], dtype=jnp.int32)
        same = same & (lane[:, None] != lane[None, :])
    return jnp.max(jnp.where(same, score, floor_value), axis=1)


def prepare_kernel(emb_ref, lrow_ref, out_ref, slot_ref, *, groups, capacity):
    rows, width = emb_ref.shape
    slots = groups * capacity
    shift = CPO.bit_length() - 1
    e = emb_ref[...]
    norm = jnp.sqrt(jnp.sum(e * e, axis=1, keepdims=True) + 1e-06)
    unit = (e * (1.0 / norm)).astype(jnp.bfloat16)
    lrow = lrow_ref[...]
    orow = lax.shift_right_logical(lrow, shift)
    first = lax.broadcasted_iota(jnp.int32, (rows, rows), 0)
    second = lax.broadcasted_iota(jnp.int32, (rows, rows), 1)
    diagonal = first == second
    lcol = jnp.sum(jnp.where(diagonal, lrow, 0), axis=1, keepdims=True)
    ocol = lax.shift_right_logical(lcol, shift)
    same = ocol == orow
    rank_row = jnp.sum(jnp.where(same & (first < second), 1, 0), axis=0, keepdims=True)
    slot_row = orow * capacity + rank_row
    slot_ref[...] = slot_row
    place = (lax.broadcasted_iota(jnp.int32, (slots, rows), 0) == slot_row).astype(jnp.bfloat16)
    out_ref[:, :width] = jnp.dot(place, unit, preferred_element_type=jnp.float32).astype(jnp.bfloat16)
    tag_source = jnp.where(
        lax.broadcasted_iota(jnp.int32, (rows, 128), 1) == 0, jnp.bitwise_and(lcol, CPO - 1) + 1, 0
    ).astype(jnp.bfloat16)
    tags = jnp.dot(place, tag_source, preferred_element_type=jnp.float32) - 1.0
    out_ref[:, width:] = tags.astype(jnp.bfloat16)


def prepare(embeddings, labels, groups, capacity):
    rows, width = embeddings.shape
    slots = groups * capacity
    vmem = pltpu.MemorySpace.VMEM
    return pl.pallas_call(
        functools.partial(prepare_kernel, groups=groups, capacity=capacity),
        out_shape=(
            jax.ShapeDtypeStruct((slots, width + 128), jnp.bfloat16),
            jax.ShapeDtypeStruct((1, rows), jnp.int32),
        ),
        in_specs=[pl.BlockSpec(memory_space=vmem)] * 2,
        out_specs=(pl.BlockSpec(memory_space=vmem), pl.BlockSpec(memory_space=vmem)),
        cost_estimate=pl.CostEstimate(
            flops=2 * slots * rows * (width + 128) + 4 * rows * width,
            transcendentals=rows,
            bytes_accessed=rows * width * 4 + slots * (width + 128) * 2,
        ),
    )(embeddings, labels[None, :])


def shards(embeddings, labels):
    rows, width = embeddings.shape
    groups = lax.axis_size("dp")
    peers = lax.axis_size("pair")
    capacity = 5 * rows // (2 * groups)
    slots = groups * capacity
    if groups <= 16:
        outgoing, slot = prepare(embeddings, labels, groups, capacity)
        slot = slot.reshape(rows)
    else:
        norm = jnp.sqrt(jnp.sum(embeddings * embeddings, axis=1, keepdims=True) + 1e-06)
        unit = (embeddings / norm).astype(jnp.bfloat16)
        owner = lax.shift_right_logical(labels, CPO.bit_length() - 1)
        local = jnp.bitwise_and(labels, CPO - 1)
        onehot = (owner[:, None] == jnp.arange(groups, dtype=jnp.int32)[None, :]).astype(jnp.int32)
        rank = jnp.sum(jnp.cumsum(onehot, axis=0) * onehot, axis=1) - 1
        slot = owner * capacity + rank
        tag_source = jnp.zeros((rows, 128), jnp.bfloat16).at[:, 0].set((local + 1).astype(jnp.bfloat16))
        source = jnp.concatenate([unit, tag_source], axis=1)
        place = slot[None, :] == jnp.arange(slots, dtype=jnp.int32)[:, None]
        outgoing = jnp.dot(place.astype(jnp.bfloat16), source, preferred_element_type=jnp.float32)
        outgoing = (outgoing - jnp.where(jnp.arange(width + 128) >= width, 1.0, 0.0)).astype(jnp.bfloat16)
    place = slot[None, :] == jnp.arange(slots, dtype=jnp.int32)[:, None]
    outgoing = outgoing.reshape(groups, capacity, width + 128)
    block = lax.all_to_all(outgoing, "dp", split_axis=0, concat_axis=0, tiled=True)
    block = block.reshape(slots, width + 128)
    top = peers // 2
    own = (block[:, :width], block[:, width])
    far = lax.ppermute(own, "pair", [(p, p ^ top) for p in range(peers)]) if top else None

    def spread(x):
        pieces = [x]
        bit = top // 2
        while bit >= 1:
            perm = [(p, p ^ bit) for p in range(peers)]
            pieces = pieces + [lax.ppermute(y, "pair", perm) for y in pieces]
            bit //= 2
        return pieces

    left, left_tags = own
    left_labels = left_tags.astype(jnp.int32)

    def best_over(pieces, first_is_own):
        best = None
        for index, (right, right_tags) in enumerate(pieces):
            piece_max = piece_best(
                left, left_labels, right, right_tags.astype(jnp.int32), first_is_own and index == 0
            )
            best = piece_max if best is None else jnp.maximum(best, piece_max)
        return best

    best = best_over(spread(own), True)
    if far is not None:
        far, best = lax.optimization_barrier((far, best))
        best = jnp.maximum(best, best_over(spread(far), False))
    place, best = lax.optimization_barrier((place, best))
    lanes = -(-capacity // 128) * 128
    sent = jnp.pad(best.reshape(groups, 1, capacity), ((0, 0), (0, 7), (0, lanes - capacity)))
    returned = lax.all_to_all(sent, "dp", split_axis=0, concat_axis=0, tiled=True)
    returned = returned[:, 0, :capacity].reshape(slots)
    return jnp.sum(jnp.where(place, returned[:, None], 0.0), axis=0)


def solution(mesh):
    in_specs = (P(("dp", "pair"), None), P(("dp", "pair")))
    out_specs = P(("dp", "pair"))
    return jax.shard_map(shards, mesh=mesh, in_specs=in_specs, out_specs=out_specs, check_vma=False)
```

```python
import functools

import jax
import jax.numpy as jnp
from jax import lax
from jax.experimental import pallas as pl
from jax.experimental.pallas import tpu as pltpu
from jax.sharding import PartitionSpec as P

CPO = 4


floor_value = -2.0


def piece_best(left, left_labels, right, right_labels, exclude_self):
    score = jnp.einsum("id,jd->ij", left, right, preferred_element_type=jnp.float32)
    same = (left_labels[:, None] == right_labels[None, :]) & (left_labels[:, None] >= 0)
    if exclude_self:
        lane = jnp.arange(left.shape[0], dtype=jnp.int32)
        same = same & (lane[:, None] != lane[None, :])
    return jnp.max(jnp.where(same, score, floor_value), axis=1)


def prepare_kernel(emb_ref, lrow_ref, out_ref, slot_ref, *, groups, capacity):
    rows, width = emb_ref.shape
    slots = groups * capacity
    shift = CPO.bit_length() - 1
    e = emb_ref[...]
    norm = jnp.sqrt(jnp.sum(e * e, axis=1, keepdims=True) + 1e-06)
    unit = (e * (1.0 / norm)).astype(jnp.bfloat16)
    lrow = lrow_ref[...]
    orow = lax.shift_right_logical(lrow, shift)
    first = lax.broadcasted_iota(jnp.int32, (rows, rows), 0)
    second = lax.broadcasted_iota(jnp.int32, (rows, rows), 1)
    diagonal = first == second
    lcol = jnp.sum(jnp.where(diagonal, lrow, 0), axis=1, keepdims=True)
    ocol = lax.shift_right_logical(lcol, shift)
    same = ocol == orow
    rank_row = jnp.sum(jnp.where(same & (first < second), 1, 0), axis=0, keepdims=True)
    slot_row = orow * capacity + rank_row
    slot_ref[...] = slot_row
    place = (lax.broadcasted_iota(jnp.int32, (slots, rows), 0) == slot_row).astype(jnp.bfloat16)
    out_ref[:, :width] = jnp.dot(place, unit, preferred_element_type=jnp.float32).astype(jnp.bfloat16)
    tag_source = jnp.where(
        lax.broadcasted_iota(jnp.int32, (rows, 128), 1) == 0, jnp.bitwise_and(lcol, CPO - 1) + 1, 0
    ).astype(jnp.bfloat16)
    tags = jnp.dot(place, tag_source, preferred_element_type=jnp.float32) - 1.0
    out_ref[:, width:] = tags.astype(jnp.bfloat16)


def prepare(embeddings, labels, groups, capacity):
    rows, width = embeddings.shape
    slots = groups * capacity
    vmem = pltpu.MemorySpace.VMEM
    return pl.pallas_call(
        functools.partial(prepare_kernel, groups=groups, capacity=capacity),
        out_shape=(
            jax.ShapeDtypeStruct((slots, width + 128), jnp.bfloat16),
            jax.ShapeDtypeStruct((1, rows), jnp.int32),
        ),
        in_specs=[pl.BlockSpec(memory_space=vmem)] * 2,
        out_specs=(pl.BlockSpec(memory_space=vmem), pl.BlockSpec(memory_space=vmem)),
        cost_estimate=pl.CostEstimate(
            flops=2 * slots * rows * (width + 128) + 4 * rows * width,
            transcendentals=rows,
            bytes_accessed=rows * width * 4 + slots * (width + 128) * 2,
        ),
    )(embeddings, labels[None, :])


def shards(embeddings, labels):
    rows, width = embeddings.shape
    groups = lax.axis_size("dp")
    peers = lax.axis_size("pair")
    capacity = 5 * rows // (2 * groups)
    slots = groups * capacity
    if groups <= 16:
        outgoing, slot = prepare(embeddings, labels, groups, capacity)
        slot = slot.reshape(rows)
    else:
        norm = jnp.sqrt(jnp.sum(embeddings * embeddings, axis=1, keepdims=True) + 1e-06)
        unit = (embeddings / norm).astype(jnp.bfloat16)
        owner = lax.shift_right_logical(labels, CPO.bit_length() - 1)
        local = jnp.bitwise_and(labels, CPO - 1)
        onehot = (owner[:, None] == jnp.arange(groups, dtype=jnp.int32)[None, :]).astype(jnp.int32)
        rank = jnp.sum(jnp.cumsum(onehot, axis=0) * onehot, axis=1) - 1
        slot = owner * capacity + rank
        tag_source = jnp.zeros((rows, 128), jnp.bfloat16).at[:, 0].set((local + 1).astype(jnp.bfloat16))
        source = jnp.concatenate([unit, tag_source], axis=1)
        place = slot[None, :] == jnp.arange(slots, dtype=jnp.int32)[:, None]
        outgoing = jnp.dot(place.astype(jnp.bfloat16), source, preferred_element_type=jnp.float32)
        outgoing = (outgoing - jnp.where(jnp.arange(width + 128) >= width, 1.0, 0.0)).astype(jnp.bfloat16)
    place = slot[None, :] == jnp.arange(slots, dtype=jnp.int32)[:, None]
    outgoing = outgoing.reshape(groups, capacity, width + 128)
    block = lax.all_to_all(outgoing, "dp", split_axis=0, concat_axis=0, tiled=True)
    block = block.reshape(slots, width + 128)
    top = peers // 2
    own = (block[:, :width], block[:, width])
    far = lax.ppermute(own, "pair", [(p, p ^ top) for p in range(peers)]) if top else None

    def spread(x):
        pieces = [x]
        bit = top // 2
        while bit >= 1:
            perm = [(p, p ^ bit) for p in range(peers)]
            pieces = pieces + [lax.ppermute(y, "pair", perm) for y in pieces]
            bit //= 2
        return pieces

    left, left_tags = own
    left_labels = left_tags.astype(jnp.int32)

    def best_over(pieces, first_is_own):
        best = None
        for index, (right, right_tags) in enumerate(pieces):
            piece_max = piece_best(
                left, left_labels, right, right_tags.astype(jnp.int32), first_is_own and index == 0
            )
            best = piece_max if best is None else jnp.maximum(best, piece_max)
        return best

    best = best_over(spread(own), True)
    if far is not None:
        far, best = lax.optimization_barrier((far, best))
        half = slots // 2
        for part in (slice(0, half), slice(half, slots)):
            rows_part = (far[0][part], far[1][part])
            best = jnp.maximum(best, best_over(spread(rows_part), False))
    place, best = lax.optimization_barrier((place, best))
    lanes = -(-capacity // 128) * 128
    sent = jnp.pad(best.reshape(groups, 1, capacity), ((0, 0), (0, 7), (0, lanes - capacity)))
    returned = lax.all_to_all(sent, "dp", split_axis=0, concat_axis=0, tiled=True)
    returned = returned[:, 0, :capacity].reshape(slots)
    return jnp.sum(jnp.where(place, returned[:, None], 0.0), axis=0)


def solution(mesh):
    in_specs = (P(("dp", "pair"), None), P(("dp", "pair")))
    out_specs = P(("dp", "pair"))
    return jax.shard_map(shards, mesh=mesh, in_specs=in_specs, out_specs=out_specs, check_vma=False)
```

```python
import functools

import jax
import jax.numpy as jnp
from jax import lax
from jax.experimental import pallas as pl
from jax.experimental.pallas import tpu as pltpu
from jax.sharding import PartitionSpec as P

CPO = 4


floor_value = -2.0


def piece_best(left, left_labels, right, right_labels, exclude_self):
    score = jnp.einsum("id,jd->ij", left, right, preferred_element_type=jnp.float32)
    same = (left_labels[:, None] == right_labels[None, :]) & (left_labels[:, None] >= 0)
    if exclude_self:
        lane = jnp.arange(left.shape[0], dtype=jnp.int32)
        same = same & (lane[:, None] != lane[None, :])
    return jnp.max(jnp.where(same, score, floor_value), axis=1)


def prepare_kernel(emb_ref, lrow_ref, out_ref, slot_ref, *, groups, capacity):
    rows, width = emb_ref.shape
    slots = groups * capacity
    shift = CPO.bit_length() - 1
    e = emb_ref[...]
    norm = jnp.sqrt(jnp.sum(e * e, axis=1, keepdims=True) + 1e-06)
    unit = (e * (1.0 / norm)).astype(jnp.bfloat16)
    lrow = lrow_ref[...]
    orow = lax.shift_right_logical(lrow, shift)
    first = lax.broadcasted_iota(jnp.int32, (rows, rows), 0)
    second = lax.broadcasted_iota(jnp.int32, (rows, rows), 1)
    diagonal = first == second
    lcol = jnp.sum(jnp.where(diagonal, lrow, 0), axis=1, keepdims=True)
    ocol = lax.shift_right_logical(lcol, shift)
    same = ocol == orow
    rank_row = jnp.sum(jnp.where(same & (first < second), 1, 0), axis=0, keepdims=True)
    slot_row = orow * capacity + rank_row
    slot_ref[...] = slot_row
    place = (lax.broadcasted_iota(jnp.int32, (slots, rows), 0) == slot_row).astype(jnp.bfloat16)
    out_ref[:, :width] = jnp.dot(place, unit, preferred_element_type=jnp.float32).astype(jnp.bfloat16)
    tag_source = jnp.where(
        lax.broadcasted_iota(jnp.int32, (rows, 128), 1) == 0, jnp.bitwise_and(lcol, CPO - 1) + 1, 0
    ).astype(jnp.bfloat16)
    tags = jnp.dot(place, tag_source, preferred_element_type=jnp.float32) - 1.0
    out_ref[:, width:] = tags.astype(jnp.bfloat16)


def prepare(embeddings, labels, groups, capacity):
    rows, width = embeddings.shape
    slots = groups * capacity
    vmem = pltpu.MemorySpace.VMEM
    return pl.pallas_call(
        functools.partial(prepare_kernel, groups=groups, capacity=capacity),
        out_shape=(
            jax.ShapeDtypeStruct((slots, width + 128), jnp.bfloat16),
            jax.ShapeDtypeStruct((1, rows), jnp.int32),
        ),
        in_specs=[pl.BlockSpec(memory_space=vmem)] * 2,
        out_specs=(pl.BlockSpec(memory_space=vmem), pl.BlockSpec(memory_space=vmem)),
        cost_estimate=pl.CostEstimate(
            flops=2 * slots * rows * (width + 128) + 4 * rows * width,
            transcendentals=rows,
            bytes_accessed=rows * width * 4 + slots * (width + 128) * 2,
        ),
    )(embeddings, labels[None, :])


def shards(embeddings, labels):
    rows, width = embeddings.shape
    groups = lax.axis_size("dp")
    peers = lax.axis_size("pair")
    capacity = 5 * rows // (2 * groups)
    slots = groups * capacity
    if groups <= 16:
        outgoing, slot = prepare(embeddings, labels, groups, capacity)
        slot = slot.reshape(rows)
    else:
        norm = jnp.sqrt(jnp.sum(embeddings * embeddings, axis=1, keepdims=True) + 1e-06)
        unit = (embeddings / norm).astype(jnp.bfloat16)
        owner = lax.shift_right_logical(labels, CPO.bit_length() - 1)
        local = jnp.bitwise_and(labels, CPO - 1)
        onehot = (owner[:, None] == jnp.arange(groups, dtype=jnp.int32)[None, :]).astype(jnp.int32)
        rank = jnp.sum(jnp.cumsum(onehot, axis=0) * onehot, axis=1) - 1
        slot = owner * capacity + rank
        tag_source = jnp.zeros((rows, 128), jnp.bfloat16).at[:, 0].set((local + 1).astype(jnp.bfloat16))
        source = jnp.concatenate([unit, tag_source], axis=1)
        place = slot[None, :] == jnp.arange(slots, dtype=jnp.int32)[:, None]
        outgoing = jnp.dot(place.astype(jnp.bfloat16), source, preferred_element_type=jnp.float32)
        outgoing = (outgoing - jnp.where(jnp.arange(width + 128) >= width, 1.0, 0.0)).astype(jnp.bfloat16)
    place = slot[None, :] == jnp.arange(slots, dtype=jnp.int32)[:, None]
    outgoing = outgoing.reshape(groups, capacity, width + 128)
    block = lax.all_to_all(outgoing, "dp", split_axis=0, concat_axis=0, tiled=True)
    block = block.reshape(slots, width + 128)
    top = peers // 2
    own = (block[:, :width], block[:, width])
    far = lax.ppermute(own, "pair", [(p, p ^ top) for p in range(peers)]) if top else None

    def spread(x):
        pieces = [x]
        bit = top // 2
        while bit >= 1:
            perm = [(p, p ^ bit) for p in range(peers)]
            pieces = pieces + [lax.ppermute(y, "pair", perm) for y in pieces]
            bit //= 2
        return pieces

    left, left_tags = own
    left_labels = left_tags.astype(jnp.int32)

    def best_over(pieces, first_is_own):
        best = None
        for index, (right, right_tags) in enumerate(pieces):
            piece_max = piece_best(
                left, left_labels, right, right_tags.astype(jnp.int32), first_is_own and index == 0
            )
            best = piece_max if best is None else jnp.maximum(best, piece_max)
        return best

    best = best_over(spread(own), True)
    if far is not None:
        far, best = lax.optimization_barrier((far, best))
        best = jnp.maximum(best, best_over(spread(far), False))
    place, best = lax.optimization_barrier((place, best))
    lanes = -(-capacity // 128) * 128
    sent = jnp.pad(best.reshape(groups, 1, capacity), ((0, 0), (0, 7), (0, lanes - capacity)))
    returned = lax.all_to_all(sent, "dp", split_axis=0, concat_axis=0, tiled=True)
    returned = returned[:, 0, :capacity].reshape(slots)
    return jnp.dot(
        returned[None, :], place.astype(jnp.float32), precision=lax.Precision.HIGHEST
    ).reshape(rows)


def solution(mesh):
    in_specs = (P(("dp", "pair"), None), P(("dp", "pair")))
    out_specs = P(("dp", "pair"))
    return jax.shard_map(shards, mesh=mesh, in_specs=in_specs, out_specs=out_specs, check_vma=False)
```
